128 devices in a mesh: blk: 8 (over y_hi, z), group: 16 (over y_lo, x, core).
Axes of the slice: x: 4, y: 4 (y_hi: 2, y_lo: 2; y = y_hi * 2 + y_lo), z: 4, core: 2. Of those that a mesh axis runs over, the one named last changes fastest.
Arguments:
- positions: float32 [3, 1048576], P(None, ('blk', 'group')), may hold values from -6 to 6
- velocities: float32 [3, 1048576], P(None, ('blk', 'group')), may hold values from -6 to 6
- accelerations: float32 [3, 1048576], P(None, ('blk', 'group')), may hold values from -6 to 6
- jerk_rates: float32 [3, 1048576], P(None, ('blk', 'group')), may hold values from -24 to 24
- masses: float32 [1048576], P(('blk', 'group')), may hold values from 0.1 to 10
- elapsed_time: float32 [1048576], P(('blk', 'group')), may hold values from 0.05 to 0.5
- active_index: int32 [2048], P(('blk', 'group')), may hold values from 0 to 1048575
Outputs:
- new_pos: float32 [3, 2048], P(None, ('blk', 'group'))
- new_vel: float32 [3, 2048], P(None, ('blk', 'group'))
- new_acc: float32 [3, 2048], P(None, ('blk', 'group'))
- new_jerk: float32 [3, 2048], P(None, ('blk', 'group'))
The draws below stay inside these ranges and needn't reach their ends.
All inputs are finite; a program needn't handle non-finite values.
Results may differ from the reference program's by a relative error of at most 0.0003.
Values sent between devices are 32-bit elements; how exact they have to be, the bound alone decides.
No kernel may reach another device: no remote copies, remote signals or barrier semaphores. Data moves between devices by JAX's collectives and lax.ppermute only.
A program may use at most 128 MiB of HBM per device.

```python
import math
import jax
import jax.numpy as jnp
import numpy as np
from jax import lax

STARS = 1048576
ACTIVE = 2048


def touch_ends(drawn, own_key, smallest, top_value):
    longest = drawn.shape.index(max(drawn.shape))
    spots = []
    for shift in (0, 1):
        where = [jax.random.randint(jax.random.fold_in(own_key, axis), (), 0, length) for axis, length in enumerate(drawn.shape)]
        where[longest] = (where[longest] + shift) % drawn.shape[longest]
        spots.append(tuple(where))
    return drawn.at[spots[0]].set(smallest).at[spots[1]].set(top_value)


def block_scale(stream_key, dims, split, low, top_value):
    factor_of = 1.0
    for dim, shards_of in split:
        steps = jax.random.uniform(jax.random.fold_in(jax.random.fold_in(stream_key, 6), dim), (shards_of,), jnp.float32, low / len(split), top_value / len(split))
        factor_of = factor_of * jnp.repeat(jnp.exp(steps), dims[dim] // shards_of).reshape((-1,) + (1,) * (len(dims) - 1 - dim))
    return factor_of


def skewed_wide(rng, dims, count, skew):
    weights = [min(1 << octave, count + 1 - (1 << octave)) * (1 << 20) // math.isqrt((1 << octave) ** skew) + 1 for octave in range((count + 1).bit_length()) if 1 << octave <= count]
    scale = 1 + sum(weights) // (1 << 30)
    listing = np.cumsum(np.array([max(1, weight // scale) for weight in weights]))
    lot = jax.random.randint(jax.random.fold_in(rng, 1), dims, 0, int(listing[len(weights) - 1]))
    start = jnp.left_shift(1, jnp.searchsorted(jnp.asarray(listing, jnp.int32), lot, side="right").astype(jnp.int32))
    grade = start - 1 + jax.random.randint(jax.random.fold_in(rng, 4), dims, 0, 1 << 30) % jnp.minimum(start, count + 1 - start)
    return jax.random.permutation(jax.random.fold_in(rng, 2), count)[grade].astype(jnp.int32)


def scatter_about(own_key, extent, deviation, bound, split=(), held_as=jnp.bfloat16):
    gain = block_scale(own_key, extent, split, -0.22, 0.18) if split else 1.0
    values = jax.random.normal(own_key, extent, jnp.float32) * deviation * gain
    return jnp.minimum(jnp.maximum(values, -bound), bound).astype(held_as)


def setup_inputs(seed: int = 0) -> dict:
    key_list = jax.random.split(jax.random.key(seed), 8)
    positions = scatter_about(key_list[0], (3, STARS), 1.0, 6.0, ((1, 128),), jnp.float32)
    velocities = scatter_about(key_list[1], (3, STARS), 1.0, 6.0, ((1, 128),), jnp.float32)
    accelerations = scatter_about(key_list[2], (3, STARS), 1.0, 6.0, ((1, 128),), jnp.float32)
    jerk_rates = scatter_about(key_list[3], (3, STARS), 4.0, 24.0, ((1, 128),), jnp.float32)
    masses = jnp.clip(jnp.exp(math.log(10.0) - 4.6051702 * jax.random.uniform(key_list[4], (STARS,), jnp.float32) ** block_scale(key_list[4], (STARS,), ((0, 128),), -0.2, 0.2)), 0.1, 10.0)
    elapsed_time = jnp.clip(jnp.exp(math.log(0.5) - 2.3025851 * jax.random.uniform(key_list[5], (STARS,), jnp.float32) ** block_scale(key_list[5], (STARS,), ((0, 128),), -0.2, 0.2)), 0.05, 0.5)
    active_index = touch_ends(skewed_wide(key_list[6], (ACTIVE,), STARS, 1), jax.random.fold_in(key_list[6], 3), 0, STARS - 1).astype(jnp.int32)
    return dict(positions=positions, velocities=velocities, accelerations=accelerations, jerk_rates=jerk_rates, masses=masses, elapsed_time=elapsed_time, active_index=active_index)


softening = 0.001

def predict(pos_now, vel_now, acc_now, jerk_now, elapsed):
    pred_pos = pos_now + elapsed * (vel_now + elapsed * (0.5 * acc_now + elapsed * (jerk_now / 6.0)))
    pred_vel = vel_now + elapsed * (acc_now + elapsed * (0.5 * jerk_now))
    return (pred_pos, pred_vel)

def block_forces(active_data, field_piece):
    offset = field_piece[0:3, None, :] - active_data[0:3, :, None]
    motion = field_piece[3:6, None, :] - active_data[3:6, :, None]
    dist_sq = lax.optimization_barrier(jnp.sum(offset * offset, axis=0)) + softening
    inverse = lax.rsqrt(dist_sq)
    weight = field_piece[6][None, :] * inverse * inverse * inverse
    factor = 3.0 * lax.optimization_barrier(jnp.sum(offset * motion, axis=0)) / dist_sq
    accel_part = lax.optimization_barrier(jnp.sum(offset * weight, axis=2))
    jerk_part = lax.optimization_barrier(jnp.sum((motion - factor * offset) * weight, axis=2))
    return jnp.concatenate([accel_part, jerk_part], axis=0)

def pair_forces(active_data, field):
    num_active = active_data.shape[1]
    num_field = field.shape[1]
    columns = math.gcd(num_field, max(1, 524288 // num_active))

    def advance(summed, which):
        field_piece = lax.dynamic_slice_in_dim(field, (which * columns).astype(jnp.int32), columns, 1)
        return (summed + block_forces(active_data, field_piece), None)
    summed, _ = lax.scan(advance, jnp.zeros((6, num_active), jnp.float32), jnp.arange(num_field // columns, dtype=jnp.int32))
    return summed

def corrector(owner_rows, forces):
    old_pos = owner_rows[0:3]
    old_vel = owner_rows[3:6]
    old_acc = owner_rows[6:9]
    old_jerk = owner_rows[9:12]
    elapsed = owner_rows[12]
    new_acc = forces[0:3]
    new_jerk = forces[3:6]
    squared = elapsed * elapsed / 12.0
    new_vel = old_vel + 0.5 * elapsed * (old_acc + new_acc) + squared * (old_jerk - new_jerk)
    new_pos = old_pos + 0.5 * elapsed * (old_vel + new_vel) + squared * (old_acc - new_acc)
    return (new_pos, new_vel, new_acc, new_jerk)

def active_state(owner_rows):
    pred_pos, pred_vel = predict(owner_rows[0:3], owner_rows[3:6], owner_rows[6:9], owner_rows[9:12], owner_rows[12])
    return jnp.concatenate([pred_pos, pred_vel], axis=0)

def reference(positions, velocities, accelerations, jerk_rates, masses, elapsed_time, active_index):
    pred_pos, pred_vel = predict(positions, velocities, accelerations, jerk_rates, elapsed_time)
    field = jnp.concatenate([pred_pos, pred_vel, masses[None, :]], axis=0)
    packed = jnp.concatenate([positions, velocities, accelerations, jerk_rates, elapsed_time[None, :]], axis=0)
    owner_rows = jnp.take(packed, active_index.astype(jnp.int32), axis=1)
    forces = pair_forces(active_state(owner_rows), field) * (1.0 / STARS)
    return corrector(owner_rows, forces)
```

```python
import functools

import jax
import jax.numpy as jnp
from jax import lax
from jax.experimental import pallas as pl
from jax.experimental.pallas import tpu as pltpu
from jax.sharding import PartitionSpec as P

softening = 0.001
ALL = ("blk", "group")
LEVELS = (("core", 1, 2), ("x", 2, 4), ("y_lo", 8, 2), ("z", 16, 4), ("y_hi", 64, 2))
SUB = 2


def predict(pos_now, vel_now, acc_now, jerk_now, elapsed):
    pred_pos = pos_now + elapsed * (
        vel_now + elapsed * (0.5 * acc_now + elapsed * (jerk_now / 6.0))
    )
    pred_vel = vel_now + elapsed * (acc_now + elapsed * (0.5 * jerk_now))
    return (pred_pos, pred_vel)


def corrector(owner_rows, forces):
    old_pos = owner_rows[0:3]
    old_vel = owner_rows[3:6]
    old_acc = owner_rows[6:9]
    old_jerk = owner_rows[9:12]
    elapsed = owner_rows[12]
    new_acc = forces[0:3]
    new_jerk = forces[3:6]
    squared = elapsed * elapsed / 12.0
    new_vel = old_vel + 0.5 * elapsed * (old_acc + new_acc) + squared * (old_jerk - new_jerk)
    new_pos = old_pos + 0.5 * elapsed * (old_vel + new_vel) + squared * (old_acc - new_acc)
    return (new_pos, new_vel, new_acc, new_jerk)


def _perm(stride, size, shift, ndev):
    pairs = []
    for d in range(ndev):
        c = (d // stride) % size
        pairs.append((d, d + (((c + shift) % size) - c) * stride))
    return pairs


def _coord(stride, size):
    return (lax.axis_index(ALL) // stride) % size


def gather_level(x, level, ndev):
    _, stride, size = level
    parts = [x] + [lax.ppermute(x, ALL, _perm(stride, size, s, ndev)) for s in range(1, size)]
    stack = jnp.stack(parts, axis=0)
    c = _coord(stride, size)
    order = (c - jnp.arange(size)) % size
    picked = jnp.take(stack, order, axis=0)
    picked = jnp.moveaxis(picked, 0, -2)
    return picked.reshape(x.shape[:-1] + (size * x.shape[-1],))


def reduce_level(x, level, ndev):
    _, stride, size = level
    m = x.shape[-1] // size
    blocks = x.reshape(x.shape[:-1] + (size, m))
    blocks = jnp.moveaxis(blocks, -2, 0)
    c = _coord(stride, size)
    total = jnp.take(blocks, c, axis=0)
    for s in range(1, size):
        piece = jnp.take(blocks, (c + s) % size, axis=0)
        total = total + lax.ppermute(piece, ALL, _perm(stride, size, s, ndev))
    return total


def sum_level(x, level, ndev):
    _, stride, size = level
    total = x
    for s in range(1, size):
        total = total + lax.ppermute(x, ALL, _perm(stride, size, s, ndev))
    return total


def forces_kernel(act_ref, fld_ref, out_ref):
    num_k = act_ref.shape[0]
    num_j = fld_ref.shape[2]
    step_k = 8 * SUB

    def kblock(kb, carry):
        k0 = pl.multiple_of(kb * step_k, step_k)
        acts = []
        for s in range(SUB):
            a = act_ref[pl.ds(k0 + 8 * s, 8), :]
            acts.append([jnp.broadcast_to(a[:, c:c + 1], (8, 128)) for c in range(6)])

        def jstep(jc, accs):
            j0 = pl.multiple_of(jc * 128, 128)
            f = [fld_ref[c, :, pl.ds(j0, 128)] for c in range(7)]
            new = []
            for s in range(SUB):
                ax, ay, az, avx, avy, avz = acts[s]
                dx = f[0] - ax
                dy = f[1] - ay
                dz = f[2] - az
                mx = f[3] - avx
                my = f[4] - avy
                mz = f[5] - avz
                dist_sq = dx * dx + dy * dy + dz * dz + softening
                inverse = lax.rsqrt(dist_sq)
                inv2 = inverse * inverse
                weight = f[6] * inv2 * inverse
                factor = 3.0 * (dx * mx + dy * my + dz * mz) * inv2
                a6 = accs[s]
                new.append((
                    a6[0] + dx * weight,
                    a6[1] + dy * weight,
                    a6[2] + dz * weight,
                    a6[3] + (mx - factor * dx) * weight,
                    a6[4] + (my - factor * dy) * weight,
                    a6[5] + (mz - factor * dz) * weight,
                ))
            return tuple(new)

        zero = jnp.zeros((8, 128), jnp.float32)
        init = tuple(tuple(zero for _ in range(6)) for _ in range(SUB))
        accs = lax.fori_loop(0, num_j // 128, jstep, init, unroll=2)
        for s in range(SUB):
            for c in range(6):
                out_ref[pl.ds(k0 + 8 * s, 8), c:c + 1] = jnp.sum(accs[s][c], axis=1, keepdims=True)
        return carry

    lax.fori_loop(0, num_k // step_k, kblock, 0)


def pair_forces(active_t, field_b):
    num_k = active_t.shape[0]
    return pl.pallas_call(
        forces_kernel,
        out_shape=jax.ShapeDtypeStruct((num_k, 8), jnp.float32),
    )(active_t, field_b)


def on_device(positions, velocities, accelerations, jerk_rates, masses, elapsed_time, active_index):
    ndev = lax.axis_size("blk") * lax.axis_size("group")
    own_stars = positions.shape[1]
    total_stars = own_stars * ndev
    gravity = 1.0 / total_stars
    every_index = active_index
    for level in LEVELS:
        every_index = gather_level(every_index, level, ndev)
    pred_pos, pred_vel = predict(positions, velocities, accelerations, jerk_rates, elapsed_time)
    own_field = jnp.concatenate(
        [pred_pos, pred_vel, masses[None, :], jnp.zeros_like(masses)[None, :]], axis=0
    )
    field_b = jnp.broadcast_to(own_field[:, None, :], (8, 8, own_stars))
    packed = jnp.concatenate(
        [positions, velocities, accelerations, jerk_rates, elapsed_time[None, :]], axis=0
    )
    first_row = lax.axis_index(ALL) * own_stars
    local_row = every_index - first_row
    is_owned = (local_row >= 0) & (local_row < own_stars)
    picked = jnp.take(packed, jnp.clip(local_row, 0, own_stars - 1), axis=1)
    picked = jnp.where(is_owned[None, :], picked, 0.0)
    rows = picked
    for level in LEVELS:
        rows = sum_level(rows, level, ndev)
    act_pos, act_vel = predict(rows[0:3], rows[3:6], rows[6:9], rows[9:12], rows[12])
    num_k = rows.shape[1]
    active_t = jnp.concatenate(
        [act_pos, act_vel, jnp.zeros((2, num_k), jnp.float32)], axis=0
    ).T
    partial = pair_forces(active_t, field_b)[:, 0:6].T
    for level in reversed(LEVELS):
        partial = reduce_level(partial, level, ndev)
    mine = lax.axis_index(ALL) * active_index.shape[0]
    owner_rows = lax.dynamic_slice_in_dim(rows, mine, active_index.shape[0], axis=1)
    return corrector(owner_rows, partial * gravity)


def solution(mesh):
    return jax.shard_map(
        on_device,
        mesh=mesh,
        in_specs=(
            P(None, ALL),
            P(None, ALL),
            P(None, ALL),
            P(None, ALL),
            P(ALL),
            P(ALL),
            P(ALL),
        ),
        out_specs=(
            P(None, ALL),
            P(None, ALL),
            P(None, ALL),
            P(None, ALL),
        ),
        check_vma=False,
    )
```

```python
import functools

import jax
import jax.numpy as jnp
from jax import lax
from jax.experimental import pallas as pl
from jax.experimental.pallas import tpu as pltpu
from jax.sharding import PartitionSpec as P

softening = 0.001
ALL = ("blk", "group")
LEVELS = (("core", 1, 2), ("x", 2, 4), ("y_lo", 8, 2), ("z", 16, 4), ("y_hi", 64, 2))
SUB = 2


def predict(pos_now, vel_now, acc_now, jerk_now, elapsed):
    pred_pos = pos_now + elapsed * (
        vel_now + elapsed * (0.5 * acc_now + elapsed * (jerk_now / 6.0))
    )
    pred_vel = vel_now + elapsed * (acc_now + elapsed * (0.5 * jerk_now))
    return (pred_pos, pred_vel)


def corrector(owner_rows, forces):
    old_pos = owner_rows[0:3]
    old_vel = owner_rows[3:6]
    old_acc = owner_rows[6:9]
    old_jerk = owner_rows[9:12]
    elapsed = owner_rows[12]
    new_acc = forces[0:3]
    new_jerk = forces[3:6]
    squared = elapsed * elapsed / 12.0
    new_vel = old_vel + 0.5 * elapsed * (old_acc + new_acc) + squared * (old_jerk - new_jerk)
    new_pos = old_pos + 0.5 * elapsed * (old_vel + new_vel) + squared * (old_acc - new_acc)
    return (new_pos, new_vel, new_acc, new_jerk)


def _perm(stride, size, shift, ndev):
    pairs = []
    for d in range(ndev):
        c = (d // stride) % size
        pairs.append((d, d + (((c + shift) % size) - c) * stride))
    return pairs


def _coord(stride, size):
    return (lax.axis_index(ALL) // stride) % size


def gather_level(x, level, ndev):
    _, stride, size = level
    parts = [x] + [lax.ppermute(x, ALL, _perm(stride, size, s, ndev)) for s in range(1, size)]
    stack = jnp.stack(parts, axis=0)
    c = _coord(stride, size)
    order = (c - jnp.arange(size)) % size
    picked = jnp.take(stack, order, axis=0)
    picked = jnp.moveaxis(picked, 0, -2)
    return picked.reshape(x.shape[:-1] + (size * x.shape[-1],))


def reduce_level(x, level, ndev):
    _, stride, size = level
    m = x.shape[-1] // size
    blocks = x.reshape(x.shape[:-1] + (size, m))
    blocks = jnp.moveaxis(blocks, -2, 0)
    c = _coord(stride, size)
    total = jnp.take(blocks, c, axis=0)
    for s in range(1, size):
        piece = jnp.take(blocks, (c + s) % size, axis=0)
        total = total + lax.ppermute(piece, ALL, _perm(stride, size, s, ndev))
    return total


def sum_level(x, level, ndev):
    _, stride, size = level
    total = x
    for s in range(1, size):
        total = total + lax.ppermute(x, ALL, _perm(stride, size, s, ndev))
    return total


def forces_kernel(act_ref, fld_ref, out_ref):
    num_k = act_ref.shape[0]
    num_j = fld_ref.shape[2]
    step_k = 8 * SUB

    def kblock(kb, carry):
        k0 = pl.multiple_of(kb * step_k, step_k)
        acts = []
        for s in range(SUB):
            a = act_ref[pl.ds(k0 + 8 * s, 8), :]
            acts.append([jnp.broadcast_to(a[:, c:c + 1], (8, 128)) for c in range(6)])

        def jstep(jc, accs):
            j0 = pl.multiple_of(jc * 128, 128)
            f = [fld_ref[c, :, pl.ds(j0, 128)] for c in range(7)]
            new = []
            for s in range(SUB):
                ax, ay, az, avx, avy, avz = acts[s]
                dx = f[0] - ax
                dy = f[1] - ay
                dz = f[2] - az
                mx = f[3] - avx
                my = f[4] - avy
                mz = f[5] - avz
                dist_sq = dx * dx + dy * dy + dz * dz + softening
                inverse = lax.rsqrt(dist_sq)
                inv2 = inverse * inverse
                weight = f[6] * inv2 * inverse
                factor = 3.0 * (dx * mx + dy * my + dz * mz) * inv2
                a6 = accs[s]
                new.append((
                    a6[0] + dx * weight,
                    a6[1] + dy * weight,
                    a6[2] + dz * weight,
                    a6[3] + (mx - factor * dx) * weight,
                    a6[4] + (my - factor * dy) * weight,
                    a6[5] + (mz - factor * dz) * weight,
                ))
            return tuple(new)

        zero = jnp.zeros((8, 128), jnp.float32)
        init = tuple(tuple(zero for _ in range(6)) for _ in range(SUB))
        accs = lax.fori_loop(0, num_j // 128, jstep, init, unroll=8)
        for s in range(SUB):
            for c in range(6):
                out_ref[pl.ds(k0 + 8 * s, 8), c:c + 1] = jnp.sum(accs[s][c], axis=1, keepdims=True)
        return carry

    lax.fori_loop(0, num_k // step_k, kblock, 0)


def pair_forces(active_t, field_b):
    num_k = active_t.shape[0]
    return pl.pallas_call(
        forces_kernel,
        out_shape=jax.ShapeDtypeStruct((num_k, 8), jnp.float32),
    )(active_t, field_b)


def on_device(positions, velocities, accelerations, jerk_rates, masses, elapsed_time, active_index):
    ndev = lax.axis_size("blk") * lax.axis_size("group")
    own_stars = positions.shape[1]
    total_stars = own_stars * ndev
    gravity = 1.0 / total_stars
    every_index = active_index
    for level in LEVELS:
        every_index = gather_level(every_index, level, ndev)
    pred_pos, pred_vel = predict(positions, velocities, accelerations, jerk_rates, elapsed_time)
    own_field = jnp.concatenate(
        [pred_pos, pred_vel, masses[None, :], jnp.zeros_like(masses)[None, :]], axis=0
    )
    field_b = jnp.broadcast_to(own_field[:, None, :], (8, 8, own_stars))
    packed = jnp.concatenate(
        [positions, velocities, accelerations, jerk_rates, elapsed_time[None, :]], axis=0
    )
    first_row = lax.axis_index(ALL) * own_stars
    local_row = every_index - first_row
    is_owned = (local_row >= 0) & (local_row < own_stars)
    picked = jnp.take(packed, jnp.clip(local_row, 0, own_stars - 1), axis=1)
    picked = jnp.where(is_owned[None, :], picked, 0.0)
    rows = picked
    for level in LEVELS:
        rows = sum_level(rows, level, ndev)
    act_pos, act_vel = predict(rows[0:3], rows[3:6], rows[6:9], rows[9:12], rows[12])
    num_k = rows.shape[1]
    active_t = jnp.concatenate(
        [act_pos, act_vel, jnp.zeros((2, num_k), jnp.float32)], axis=0
    ).T
    partial = pair_forces(active_t, field_b)[:, 0:6].T
    for level in reversed(LEVELS):
        partial = reduce_level(partial, level, ndev)
    mine = lax.axis_index(ALL) * active_index.shape[0]
    owner_rows = lax.dynamic_slice_in_dim(rows, mine, active_index.shape[0], axis=1)
    return corrector(owner_rows, partial * gravity)


def solution(mesh):
    return jax.shard_map(
        on_device,
        mesh=mesh,
        in_specs=(
            P(None, ALL),
            P(None, ALL),
            P(None, ALL),
            P(None, ALL),
            P(ALL),
            P(ALL),
            P(ALL),
        ),
        out_specs=(
            P(None, ALL),
            P(None, ALL),
            P(None, ALL),
            P(None, ALL),
        ),
        check_vma=False,
    )
```

```python
import jax
import jax.numpy as jnp
from jax import lax
from jax.experimental import pallas as pl
from jax.experimental.pallas import tpu as pltpu
from jax.sharding import PartitionSpec as P

softening = 0.001
ALL = ("blk", "group")
SUB = 2


def predict(pos_now, vel_now, acc_now, jerk_now, elapsed):
    pred_pos = pos_now + elapsed * (
        vel_now + elapsed * (0.5 * acc_now + elapsed * (jerk_now / 6.0))
    )
    pred_vel = vel_now + elapsed * (acc_now + elapsed * (0.5 * jerk_now))
    return (pred_pos, pred_vel)


def corrector(owner_rows, forces):
    old_pos = owner_rows[0:3]
    old_vel = owner_rows[3:6]
    old_acc = owner_rows[6:9]
    old_jerk = owner_rows[9:12]
    elapsed = owner_rows[12]
    new_acc = forces[0:3]
    new_jerk = forces[3:6]
    squared = elapsed * elapsed / 12.0
    new_vel = old_vel + 0.5 * elapsed * (old_acc + new_acc) + squared * (old_jerk - new_jerk)
    new_pos = old_pos + 0.5 * elapsed * (old_vel + new_vel) + squared * (old_acc - new_acc)
    return (new_pos, new_vel, new_acc, new_jerk)


def _partner(bit, ndev):
    return [(d, d ^ (1 << bit)) for d in range(ndev)]


def _upper(bit):
    return ((lax.axis_index(ALL) >> bit) & 1) == 1


def gather_all(x, ndev):
    for bit in range(ndev.bit_length() - 1):
        recv = lax.ppermute(x, ALL, _partner(bit, ndev))
        x = jnp.where(
            _upper(bit), jnp.concatenate([recv, x], axis=-1), jnp.concatenate([x, recv], axis=-1)
        )
    return x


def sum_all(x, ndev):
    for bit in range(ndev.bit_length() - 1):
        x = x + lax.ppermute(x, ALL, _partner(bit, ndev))
    return x


def reduce_scatter_all(x, ndev):
    for bit in reversed(range(ndev.bit_length() - 1)):
        half = x.shape[-1] // 2
        low, high = x[..., :half], x[..., half:]
        upper = _upper(bit)
        keep = jnp.where(upper, high, low)
        send = jnp.where(upper, low, high)
        x = keep + lax.ppermute(send, ALL, _partner(bit, ndev))
    return x


def forces_kernel(act_ref, fld_ref, out_ref):
    num_k = act_ref.shape[0]
    num_j = fld_ref.shape[2]
    step_k = 8 * SUB

    def kblock(kb, carry):
        k0 = pl.multiple_of(kb * step_k, step_k)
        acts = []
        for s in range(SUB):
            a = act_ref[pl.ds(k0 + 8 * s, 8), :]
            acts.append([jnp.broadcast_to(a[:, c:c + 1], (8, 128)) for c in range(6)])

        def jstep(jc, accs):
            j0 = pl.multiple_of(jc * 128, 128)
            f = [fld_ref[c, :, pl.ds(j0, 128)] for c in range(7)]
            new = []
            for s in range(SUB):
                ax, ay, az, avx, avy, avz = acts[s]
                dx = f[0] - ax
                dy = f[1] - ay
                dz = f[2] - az
                mx = f[3] - avx
                my = f[4] - avy
                mz = f[5] - avz
                dist_sq = dx * dx + dy * dy + dz * dz + softening
                inverse = lax.rsqrt(dist_sq)
                inv2 = inverse * inverse
                weight = f[6] * inv2 * inverse
                factor = 3.0 * (dx * mx + dy * my + dz * mz) * inv2
                a6 = accs[s]
                new.append((
                    a6[0] + dx * weight,
                    a6[1] + dy * weight,
                    a6[2] + dz * weight,
                    a6[3] + (mx - factor * dx) * weight,
                    a6[4] + (my - factor * dy) * weight,
                    a6[5] + (mz - factor * dz) * weight,
                ))
            return tuple(new)

        zero = jnp.zeros((8, 128), jnp.float32)
        init = tuple(tuple(zero for _ in range(6)) for _ in range(SUB))
        accs = lax.fori_loop(0, num_j // 128, jstep, init, unroll=8)
        for s in range(SUB):
            for c in range(6):
                out_ref[pl.ds(k0 + 8 * s, 8), c:c + 1] = jnp.sum(accs[s][c], axis=1, keepdims=True)
        return carry

    lax.fori_loop(0, num_k // step_k, kblock, 0)


def pair_forces(active_t, field_b):
    num_k = active_t.shape[0]
    return pl.pallas_call(
        forces_kernel,
        out_shape=jax.ShapeDtypeStruct((num_k, 8), jnp.float32),
    )(active_t, field_b)


def on_device(positions, velocities, accelerations, jerk_rates, masses, elapsed_time, active_index):
    ndev = lax.axis_size("blk") * lax.axis_size("group")
    own_stars = positions.shape[1]
    total_stars = own_stars * ndev
    gravity = 1.0 / total_stars
    every_index = gather_all(active_index, ndev)
    pred_pos, pred_vel = predict(positions, velocities, accelerations, jerk_rates, elapsed_time)
    own_field = jnp.concatenate(
        [pred_pos, pred_vel, masses[None, :], jnp.zeros_like(masses)[None, :]], axis=0
    )
    field_b = jnp.broadcast_to(own_field[:, None, :], (8, 8, own_stars))
    packed = jnp.concatenate(
        [positions, velocities, accelerations, jerk_rates, elapsed_time[None, :]], axis=0
    )
    first_row = lax.axis_index(ALL) * own_stars
    local_row = every_index - first_row
    is_owned = (local_row >= 0) & (local_row < own_stars)
    picked = jnp.take(packed, jnp.clip(local_row, 0, own_stars - 1), axis=1)
    picked = jnp.where(is_owned[None, :], picked, 0.0)
    rows = sum_all(picked, ndev)
    act_pos, act_vel = predict(rows[0:3], rows[3:6], rows[6:9], rows[9:12], rows[12])
    num_k = rows.shape[1]
    active_t = jnp.concatenate(
        [act_pos, act_vel, jnp.zeros((2, num_k), jnp.float32)], axis=0
    ).T
    partial = pair_forces(active_t, field_b)[:, 0:6].T
    partial = reduce_scatter_all(partial, ndev)
    mine = lax.axis_index(ALL) * active_index.shape[0]
    owner_rows = lax.dynamic_slice_in_dim(rows, mine, active_index.shape[0], axis=1)
    return corrector(owner_rows, partial * gravity)


def solution(mesh):
    return jax.shard_map(
        on_device,
        mesh=mesh,
        in_specs=(
            P(None, ALL),
            P(None, ALL),
            P(None, ALL),
            P(None, ALL),
            P(ALL),
            P(ALL),
            P(ALL),
        ),
        out_specs=(
            P(None, ALL),
            P(None, ALL),
            P(None, ALL),
            P(None, ALL),
        ),
        check_vma=False,
    )
```

```python
import functools

import jax
import jax.numpy as jnp
from jax import lax
from jax.experimental import pallas as pl
from jax.experimental.pallas import tpu as pltpu
from jax.sharding import PartitionSpec as P

softening = 0.001
ALL = ("blk", "group")
LEVELS = (("core", 1, 2), ("x", 2, 4), ("y_lo", 8, 2), ("z", 16, 4), ("y_hi", 64, 2))
SUB = 2


def predict(pos_now, vel_now, acc_now, jerk_now, elapsed):
    pred_pos = pos_now + elapsed * (
        vel_now + elapsed * (0.5 * acc_now + elapsed * (jerk_now / 6.0))
    )
    pred_vel = vel_now + elapsed * (acc_now + elapsed * (0.5 * jerk_now))
    return (pred_pos, pred_vel)


def corrector_terms(rows):
    old_pos = rows[0:3]
    old_vel = rows[3:6]
    old_acc = rows[6:9]
    old_jerk = rows[9:12]
    elapsed = rows[12]
    half = 0.5 * elapsed
    squared = elapsed * elapsed / 12.0
    vel_part = old_vel + half * old_acc + squared * old_jerk
    pos_part = old_pos + half * old_vel + squared * old_acc
    return jnp.concatenate([pos_part, vel_part, elapsed[None, :]], axis=0)


def corrector(terms, forces):
    pos_part = terms[0:3]
    vel_part = terms[3:6]
    elapsed = terms[6]
    new_acc = forces[0:3]
    new_jerk = forces[3:6]
    half = 0.5 * elapsed
    squared = elapsed * elapsed / 12.0
    new_vel = vel_part + half * new_acc - squared * new_jerk
    new_pos = pos_part + half * new_vel - squared * new_acc
    return (new_pos, new_vel, new_acc, new_jerk)


def _perm(stride, size, shift, ndev):
    pairs = []
    for d in range(ndev):
        c = (d // stride) % size
        pairs.append((d, d + (((c + shift) % size) - c) * stride))
    return pairs


def _coord(stride, size):
    return (lax.axis_index(ALL) // stride) % size


def gather_level(x, level, ndev):
    _, stride, size = level
    parts = [x] + [lax.ppermute(x, ALL, _perm(stride, size, s, ndev)) for s in range(1, size)]
    stack = jnp.stack(parts, axis=0)
    c = _coord(stride, size)
    order = (c - jnp.arange(size)) % size
    picked = jnp.take(stack, order, axis=0)
    picked = jnp.moveaxis(picked, 0, -2)
    return picked.reshape(x.shape[:-1] + (size * x.shape[-1],))


def reduce_level(x, level, ndev):
    _, stride, size = level
    m = x.shape[-1] // size
    blocks = x.reshape(x.shape[:-1] + (size, m))
    blocks = jnp.moveaxis(blocks, -2, 0)
    c = _coord(stride, size)
    total = jnp.take(blocks, c, axis=0)
    for s in range(1, size):
        piece = jnp.take(blocks, (c + s) % size, axis=0)
        total = total + lax.ppermute(piece, ALL, _perm(stride, size, s, ndev))
    return total


def sum_level(x, level, ndev):
    _, stride, size = level
    total = x
    for s in range(1, size):
        total = total + lax.ppermute(x, ALL, _perm(stride, size, s, ndev))
    return total


def forces_kernel(act_ref, fld_ref, out_ref):
    num_k = act_ref.shape[0]
    num_j = fld_ref.shape[2]
    step_k = 8 * SUB

    def kblock(kb, carry):
        k0 = pl.multiple_of(kb * step_k, step_k)
        acts = []
        for s in range(SUB):
            a = act_ref[pl.ds(k0 + 8 * s, 8), :]
            acts.append([jnp.broadcast_to(a[:, c:c + 1], (8, 128)) for c in range(6)])

        def jstep(jc, accs):
            j0 = pl.multiple_of(jc * 128, 128)
            f = [fld_ref[c, :, pl.ds(j0, 128)] for c in range(7)]
            new = []
            for s in range(SUB):
                ax, ay, az, avx, avy, avz = acts[s]
                dx = f[0] - ax
                dy = f[1] - ay
                dz = f[2] - az
                mx = f[3] - avx
                my = f[4] - avy
                mz = f[5] - avz
                dist_sq = dx * dx + dy * dy + dz * dz + softening
                inverse = lax.rsqrt(dist_sq)
                inv2 = inverse * inverse
                weight = f[6] * inv2 * inverse
                factor = 3.0 * (dx * mx + dy * my + dz * mz) * inv2
                a6 = accs[s]
                new.append((
                    a6[0] + dx * weight,
                    a6[1] + dy * weight,
                    a6[2] + dz * weight,
                    a6[3] + (mx - factor * dx) * weight,
                    a6[4] + (my - factor * dy) * weight,
                    a6[5] + (mz - factor * dz) * weight,
                ))
            return tuple(new)

        zero = jnp.zeros((8, 128), jnp.float32)
        init = tuple(tuple(zero for _ in range(6)) for _ in range(SUB))
        accs = lax.fori_loop(0, num_j // 128, jstep, init, unroll=16)
        for s in range(SUB):
            for c in range(6):
                out_ref[pl.ds(k0 + 8 * s, 8), c:c + 1] = jnp.sum(accs[s][c], axis=1, keepdims=True)
        return carry

    lax.fori_loop(0, num_k // step_k, kblock, 0)


def pair_forces(active_t, field_b):
    num_k = active_t.shape[0]
    return pl.pallas_call(
        forces_kernel,
        out_shape=jax.ShapeDtypeStruct((num_k, 8), jnp.float32),
    )(active_t, field_b)


def on_device(positions, velocities, accelerations, jerk_rates, masses, elapsed_time, active_index):
    ndev = lax.axis_size("blk") * lax.axis_size("group")
    own_stars = positions.shape[1]
    total_stars = own_stars * ndev
    gravity = 1.0 / total_stars
    every_index = active_index
    for level in LEVELS:
        every_index = gather_level(every_index, level, ndev)
    pred_pos, pred_vel = predict(positions, velocities, accelerations, jerk_rates, elapsed_time)
    own_field = jnp.concatenate(
        [pred_pos, pred_vel, masses[None, :], jnp.zeros_like(masses)[None, :]], axis=0
    )
    field_b = jnp.broadcast_to(own_field[:, None, :], (8, 8, own_stars))
    packed = jnp.concatenate(
        [positions, velocities, accelerations, jerk_rates, elapsed_time[None, :]], axis=0
    )
    first_row = lax.axis_index(ALL) * own_stars
    local_row = every_index - first_row
    is_owned = (local_row >= 0) & (local_row < own_stars)
    picked = jnp.take(packed, jnp.clip(local_row, 0, own_stars - 1), axis=1)
    picked = jnp.where(is_owned[None, :], picked, 0.0)
    act_pos, act_vel = predict(picked[0:3], picked[3:6], picked[6:9], picked[9:12], picked[12])
    num_k = picked.shape[1]
    active = jnp.concatenate([act_pos, act_vel], axis=0)
    for level in LEVELS:
        active = sum_level(active, level, ndev)
    active_t = jnp.concatenate([active, jnp.zeros((2, num_k), jnp.float32)], axis=0).T
    partial = pair_forces(active_t, field_b)[:, 0:6].T
    payload = jnp.concatenate([partial, corrector_terms(picked)], axis=0)
    for level in reversed(LEVELS):
        payload = reduce_level(payload, level, ndev)
    return corrector(payload[6:13], payload[0:6] * gravity)


def solution(mesh):
    return jax.shard_map(
        on_device,
        mesh=mesh,
        in_specs=(
            P(None, ALL),
            P(None, ALL),
            P(None, ALL),
            P(None, ALL),
            P(ALL),
            P(ALL),
            P(ALL),
        ),
        out_specs=(
            P(None, ALL),
            P(None, ALL),
            P(None, ALL),
            P(None, ALL),
        ),
        check_vma=False,
    )
```

```python
import functools

import math

import jax
import jax.numpy as jnp
from jax import lax
from jax.experimental import pallas as pl
from jax.experimental.pallas import tpu as pltpu
from jax.sharding import PartitionSpec as P

softening = 0.001
ALL = ("blk", "group")
GROUP_LEVELS = (("core", 1, 2), ("x", 2, 4), ("y_lo", 8, 2))
BLK_LEVELS = (("z", 16, 4), ("y_hi", 64, 2))
LEVELS = GROUP_LEVELS + BLK_LEVELS
SUB = 2


def predict(pos_now, vel_now, acc_now, jerk_now, elapsed):
    pred_pos = pos_now + elapsed * (
        vel_now + elapsed * (0.5 * acc_now + elapsed * (jerk_now / 6.0))
    )
    pred_vel = vel_now + elapsed * (acc_now + elapsed * (0.5 * jerk_now))
    return (pred_pos, pred_vel)


def corrector_terms(rows):
    old_pos = rows[0:3]
    old_vel = rows[3:6]
    old_acc = rows[6:9]
    old_jerk = rows[9:12]
    elapsed = rows[12]
    half = 0.5 * elapsed
    squared = elapsed * elapsed / 12.0
    vel_part = old_vel + half * old_acc + squared * old_jerk
    pos_part = old_pos + half * old_vel + squared * old_acc
    return jnp.concatenate([pos_part, vel_part, elapsed[None, :]], axis=0)


def corrector(terms, forces):
    pos_part = terms[0:3]
    vel_part = terms[3:6]
    elapsed = terms[6]
    new_acc = forces[0:3]
    new_jerk = forces[3:6]
    half = 0.5 * elapsed
    squared = elapsed * elapsed / 12.0
    new_vel = vel_part + half * new_acc - squared * new_jerk
    new_pos = pos_part + half * new_vel - squared * new_acc
    return (new_pos, new_vel, new_acc, new_jerk)


def _perm(stride, size, shift, ndev):
    pairs = []
    for d in range(ndev):
        c = (d // stride) % size
        pairs.append((d, d + (((c + shift) % size) - c) * stride))
    return pairs


def _coord(stride, size):
    return (lax.axis_index(ALL) // stride) % size


def gather_level(x, level, ndev):
    _, stride, size = level
    parts = [x] + [lax.ppermute(x, ALL, _perm(stride, size, s, ndev)) for s in range(1, size)]
    stack = jnp.stack(parts, axis=0)
    c = _coord(stride, size)
    order = (c - jnp.arange(size)) % size
    picked = jnp.take(stack, order, axis=0)
    picked = jnp.moveaxis(picked, 0, -2)
    return picked.reshape(x.shape[:-1] + (size * x.shape[-1],))


def reduce_level(x, level, ndev):
    _, stride, size = level
    m = x.shape[-1] // size
    blocks = x.reshape(x.shape[:-1] + (size, m))
    blocks = jnp.moveaxis(blocks, -2, 0)
    c = _coord(stride, size)
    total = jnp.take(blocks, c, axis=0)
    for s in range(1, size):
        piece = jnp.take(blocks, (c + s) % size, axis=0)
        total = total + lax.ppermute(piece, ALL, _perm(stride, size, s, ndev))
    return total


def sum_level(x, level, ndev):
    _, stride, size = level
    total = x
    for s in range(1, size):
        total = total + lax.ppermute(x, ALL, _perm(stride, size, s, ndev))
    return total


def forces_kernel(act_ref, fld_ref, out_ref, bfld, acc):
    num_k = act_ref.shape[0]
    num_j = fld_ref.shape[1]
    width = bfld.shape[2]
    step_k = 8 * SUB
    acc[...] = jnp.zeros(acc.shape, jnp.float32)

    def jblock(jb, carry):
        base = pl.multiple_of(jb * width, width)

        def spread(ci, c2):
            j0 = pl.multiple_of(ci * 128, 128)
            for c in range(7):
                row = fld_ref[c:c + 1, pl.ds(base + j0, 128)]
                bfld[c, :, pl.ds(j0, 128)] = jnp.broadcast_to(row, (8, 128))
            return c2

        lax.fori_loop(0, width // 128, spread, 0, unroll=4)

        def kblock(kb, c3):
            k0 = pl.multiple_of(kb * step_k, step_k)
            acts = []
            for s in range(SUB):
                a = act_ref[pl.ds(k0 + 8 * s, 8), :]
                acts.append([jnp.broadcast_to(a[:, c:c + 1], (8, 128)) for c in range(6)])

            def jstep(jc, accs):
                j0 = pl.multiple_of(jc * 128, 128)
                f = [bfld[c, :, pl.ds(j0, 128)] for c in range(7)]
                new = []
                for s in range(SUB):
                    ax, ay, az, avx, avy, avz = acts[s]
                    dx = f[0] - ax
                    dy = f[1] - ay
                    dz = f[2] - az
                    mx = f[3] - avx
                    my = f[4] - avy
                    mz = f[5] - avz
                    dist_sq = dx * dx + dy * dy + dz * dz + softening
                    inverse = lax.rsqrt(dist_sq)
                    inv2 = inverse * inverse
                    weight = f[6] * inv2 * inverse
                    factor = 3.0 * (dx * mx + dy * my + dz * mz) * inv2
                    a6 = accs[s]
                    new.append((
                        a6[0] + dx * weight,
                        a6[1] + dy * weight,
                        a6[2] + dz * weight,
                        a6[3] + (mx - factor * dx) * weight,
                        a6[4] + (my - factor * dy) * weight,
                        a6[5] + (mz - factor * dz) * weight,
                    ))
                return tuple(new)

            slot = kb * SUB
            init = tuple(tuple(acc[slot + s, c] for c in range(6)) for s in range(SUB))
            accs = lax.fori_loop(0, width // 128, jstep, init, unroll=16)
            for s in range(SUB):
                for c in range(6):
                    acc[slot + s, c] = accs[s][c]
            return c3

        lax.fori_loop(0, num_k // step_k, kblock, 0)
        return carry

    lax.fori_loop(0, num_j // width, jblock, 0)
    for kb in range(num_k // 8):
        for c in range(6):
            out_ref[pl.ds(8 * kb, 8), c:c + 1] = jnp.sum(acc[kb, c], axis=1, keepdims=True)


def pair_forces(active_t, field):
    num_k = active_t.shape[0]
    width = math.gcd(field.shape[1], 8192)
    return pl.pallas_call(
        forces_kernel,
        out_shape=jax.ShapeDtypeStruct((num_k, 8), jnp.float32),
        scratch_shapes=[
            pltpu.VMEM((7, 8, width), jnp.float32),
            pltpu.VMEM((num_k // 8, 6, 8, 128), jnp.float32),
        ],
    )(active_t, field)


def concat_level(x, level, ndev):
    _, stride, size = level
    parts = [x] + [lax.ppermute(x, ALL, _perm(stride, size, s, ndev)) for s in range(1, size)]
    return jnp.concatenate(parts, axis=-1)


def on_device(positions, velocities, accelerations, jerk_rates, masses, elapsed_time, active_index):
    num_blk = lax.axis_size("blk")
    num_group = lax.axis_size("group")
    ndev = num_blk * num_group
    own_stars = positions.shape[1]
    own_active = active_index.shape[0]
    total_stars = own_stars * ndev
    gravity = 1.0 / total_stars
    pred_pos, pred_vel = predict(positions, velocities, accelerations, jerk_rates, elapsed_time)
    field = jnp.concatenate([pred_pos, pred_vel, masses[None, :]], axis=0)
    for level in (GROUP_LEVELS[2], GROUP_LEVELS[1], GROUP_LEVELS[0]):
        field = concat_level(field, level, ndev)
    every_index = active_index
    for level in LEVELS:
        every_index = gather_level(every_index, level, ndev)
    packed = jnp.concatenate(
        [positions, velocities, accelerations, jerk_rates, elapsed_time[None, :]], axis=0
    )
    first_row = lax.axis_index(ALL) * own_stars
    local_row = every_index - first_row
    is_owned = (local_row >= 0) & (local_row < own_stars)
    picked = jnp.take(packed, jnp.clip(local_row, 0, own_stars - 1), axis=1)
    picked = jnp.where(is_owned[None, :], picked, 0.0)
    act_pos, act_vel = predict(picked[0:3], picked[3:6], picked[6:9], picked[9:12], picked[12])
    payload = jnp.concatenate([act_pos, act_vel, corrector_terms(picked)], axis=0)
    rows = payload.shape[0]
    payload = payload.reshape(rows, num_blk, num_group, own_active)
    payload = payload.transpose(0, 2, 1, 3).reshape(rows, ndev * own_active)
    for level in reversed(GROUP_LEVELS):
        payload = reduce_level(payload, level, ndev)
    for level in BLK_LEVELS:
        payload = sum_level(payload, level, ndev)
    num_k = payload.shape[1]
    active_t = jnp.concatenate([payload[0:6], jnp.zeros((2, num_k), jnp.float32)], axis=0).T
    partial = pair_forces(active_t, field)[:, 0:6].T
    for level in reversed(BLK_LEVELS):
        partial = reduce_level(partial, level, ndev)
    mine = lax.axis_index("blk") * own_active
    terms = lax.dynamic_slice_in_dim(payload[6:13], mine, own_active, axis=1)
    return corrector(terms, partial * gravity)


def solution(mesh):
    return jax.shard_map(
        on_device,
        mesh=mesh,
        in_specs=(
            P(None, ALL),
            P(None, ALL),
            P(None, ALL),
            P(None, ALL),
            P(ALL),
            P(ALL),
            P(ALL),
        ),
        out_specs=(
            P(None, ALL),
            P(None, ALL),
            P(None, ALL),
            P(None, ALL),
        ),
        check_vma=False,
    )
```

```python
import functools

import math

import jax
import jax.numpy as jnp
from jax import lax
from jax.experimental import pallas as pl
from jax.experimental.pallas import tpu as pltpu
from jax.sharding import PartitionSpec as P

softening = 0.001
ALL = ("blk", "group")
GROUP_LEVELS = (("core", 1, 2), ("x", 2, 4), ("y_lo", 8, 2))
BLK_LEVELS = (("z", 16, 4), ("y_hi", 64, 2))
LEVELS = GROUP_LEVELS + BLK_LEVELS
SUB = 2


def predict(pos_now, vel_now, acc_now, jerk_now, elapsed):
    pred_pos = pos_now + elapsed * (
        vel_now + elapsed * (0.5 * acc_now + elapsed * (jerk_now / 6.0))
    )
    pred_vel = vel_now + elapsed * (acc_now + elapsed * (0.5 * jerk_now))
    return (pred_pos, pred_vel)


def corrector_terms(rows):
    old_pos = rows[0:3]
    old_vel = rows[3:6]
    old_acc = rows[6:9]
    old_jerk = rows[9:12]
    elapsed = rows[12]
    half = 0.5 * elapsed
    squared = elapsed * elapsed / 12.0
    vel_part = old_vel + half * old_acc + squared * old_jerk
    pos_part = old_pos + half * old_vel + squared * old_acc
    return jnp.concatenate([pos_part, vel_part, elapsed[None, :]], axis=0)


def corrector(terms, forces):
    pos_part = terms[0:3]
    vel_part = terms[3:6]
    elapsed = terms[6]
    new_acc = forces[0:3]
    new_jerk = forces[3:6]
    half = 0.5 * elapsed
    squared = elapsed * elapsed / 12.0
    new_vel = vel_part + half * new_acc - squared * new_jerk
    new_pos = pos_part + half * new_vel - squared * new_acc
    return (new_pos, new_vel, new_acc, new_jerk)


def _perm(stride, size, shift, ndev):
    pairs = []
    for d in range(ndev):
        c = (d // stride) % size
        pairs.append((d, d + (((c + shift) % size) - c) * stride))
    return pairs


def _coord(stride, size):
    return (lax.axis_index(ALL) // stride) % size


def gather_level(x, level, ndev):
    _, stride, size = level
    parts = [x] + [lax.ppermute(x, ALL, _perm(stride, size, s, ndev)) for s in range(1, size)]
    stack = jnp.stack(parts, axis=0)
    c = _coord(stride, size)
    order = (c - jnp.arange(size)) % size
    picked = jnp.take(stack, order, axis=0)
    picked = jnp.moveaxis(picked, 0, -2)
    return picked.reshape(x.shape[:-1] + (size * x.shape[-1],))


def reduce_level(x, level, ndev):
    _, stride, size = level
    m = x.shape[-1] // size
    blocks = x.reshape(x.shape[:-1] + (size, m))
    blocks = jnp.moveaxis(blocks, -2, 0)
    c = _coord(stride, size)
    total = jnp.take(blocks, c, axis=0)
    for s in range(1, size):
        piece = jnp.take(blocks, (c + s) % size, axis=0)
        total = total + lax.ppermute(piece, ALL, _perm(stride, size, s, ndev))
    return total


def sum_level(x, level, ndev):
    _, stride, size = level
    total = x
    for s in range(1, size):
        total = total + lax.ppermute(x, ALL, _perm(stride, size, s, ndev))
    return total


def forces_kernel(act_ref, fld_ref, out_ref, bfld, acc):
    num_k = act_ref.shape[0]
    num_j = fld_ref.shape[1]
    width = bfld.shape[2]
    step_k = 8 * SUB
    acc[...] = jnp.zeros(acc.shape, jnp.float32)

    def jblock(jb, carry):
        base = pl.multiple_of(jb * width, width)

        def spread(ci, c2):
            j0 = pl.multiple_of(ci * 128, 128)
            for c in range(7):
                row = fld_ref[c:c + 1, pl.ds(base + j0, 128)]
                bfld[c, :, pl.ds(j0, 128)] = jnp.broadcast_to(row, (8, 128))
            return c2

        lax.fori_loop(0, width // 128, spread, 0, unroll=4)

        def kblock(kb, c3):
            k0 = pl.multiple_of(kb * step_k, step_k)
            acts = []
            for s in range(SUB):
                a = act_ref[pl.ds(k0 + 8 * s, 8), :]
                acts.append([jnp.broadcast_to(a[:, c:c + 1], (8, 128)) for c in range(6)])

            def jstep(jc, accs):
                j0 = pl.multiple_of(jc * 128, 128)
                f = [bfld[c, :, pl.ds(j0, 128)] for c in range(7)]
                new = []
                for s in range(SUB):
                    ax, ay, az, avx, avy, avz = acts[s]
                    dx = f[0] - ax
                    dy = f[1] - ay
                    dz = f[2] - az
                    mx = f[3] - avx
                    my = f[4] - avy
                    mz = f[5] - avz
                    dist_sq = dx * dx + dy * dy + dz * dz + softening
                    inverse = lax.rsqrt(dist_sq)
                    inv2 = inverse * inverse
                    weight = f[6] * inv2 * inverse
                    factor = 3.0 * (dx * mx + dy * my + dz * mz) * inv2
                    a6 = accs[s]
                    new.append((
                        a6[0] + dx * weight,
                        a6[1] + dy * weight,
                        a6[2] + dz * weight,
                        a6[3] + (mx - factor * dx) * weight,
                        a6[4] + (my - factor * dy) * weight,
                        a6[5] + (mz - factor * dz) * weight,
                    ))
                return tuple(new)

            slot = kb * SUB
            init = tuple(tuple(acc[slot + s, c] for c in range(6)) for s in range(SUB))
            accs = lax.fori_loop(0, width // 128, jstep, init, unroll=16)
            for s in range(SUB):
                for c in range(6):
                    acc[slot + s, c] = accs[s][c]
            return c3

        lax.fori_loop(0, num_k // step_k, kblock, 0)
        return carry

    lax.fori_loop(0, num_j // width, jblock, 0)
    for kb in range(num_k // 8):
        for c in range(6):
            out_ref[pl.ds(8 * kb, 8), c:c + 1] = jnp.sum(acc[kb, c], axis=1, keepdims=True)


def pair_forces(active_t, field):
    num_k = active_t.shape[0]
    width = math.gcd(field.shape[1], 8192)
    return pl.pallas_call(
        forces_kernel,
        out_shape=jax.ShapeDtypeStruct((num_k, 8), jnp.float32),
        scratch_shapes=[
            pltpu.VMEM((7, 8, width), jnp.float32),
            pltpu.VMEM((num_k // 8, 6, 8, 128), jnp.float32),
        ],
    )(active_t, field)


def concat_level(x, level, ndev):
    _, stride, size = level
    parts = [x] + [lax.ppermute(x, ALL, _perm(stride, size, s, ndev)) for s in range(1, size)]
    return jnp.concatenate(parts, axis=-1)


def on_device(positions, velocities, accelerations, jerk_rates, masses, elapsed_time, active_index):
    num_blk = lax.axis_size("blk")
    num_group = lax.axis_size("group")
    ndev = num_blk * num_group
    own_stars = positions.shape[1]
    own_active = active_index.shape[0]
    total_stars = own_stars * ndev
    gravity = 1.0 / total_stars
    pred_pos, pred_vel = predict(positions, velocities, accelerations, jerk_rates, elapsed_time)
    field = jnp.concatenate([pred_pos, pred_vel, masses[None, :]], axis=0)
    for level in (GROUP_LEVELS[2], GROUP_LEVELS[1], GROUP_LEVELS[0]):
        field = concat_level(field, level, ndev)
    every_index = active_index
    for level in LEVELS:
        every_index = gather_level(every_index, level, ndev)
    packed = jnp.concatenate(
        [positions, velocities, accelerations, jerk_rates, elapsed_time[None, :]], axis=0
    )
    packed, field = lax.optimization_barrier((packed, field))
    first_row = lax.axis_index(ALL) * own_stars
    local_row = every_index - first_row
    is_owned = (local_row >= 0) & (local_row < own_stars)
    picked = jnp.take(packed, jnp.clip(local_row, 0, own_stars - 1), axis=1)
    picked = jnp.where(is_owned[None, :], picked, 0.0)
    act_pos, act_vel = predict(picked[0:3], picked[3:6], picked[6:9], picked[9:12], picked[12])
    payload = jnp.concatenate([act_pos, act_vel, corrector_terms(picked)], axis=0)
    rows = payload.shape[0]
    payload = payload.reshape(rows, num_blk, num_group, own_active)
    payload = payload.transpose(0, 2, 1, 3).reshape(rows, ndev * own_active)
    for level in reversed(GROUP_LEVELS):
        payload = reduce_level(payload, level, ndev)
    for level in BLK_LEVELS:
        payload = sum_level(payload, level, ndev)
    num_k = payload.shape[1]
    active_t = jnp.concatenate([payload[0:6], jnp.zeros((2, num_k), jnp.float32)], axis=0).T
    partial = pair_forces(active_t, field)[:, 0:6].T
    for level in reversed(BLK_LEVELS):
        partial = reduce_level(partial, level, ndev)
    mine = lax.axis_index("blk") * own_active
    terms = lax.dynamic_slice_in_dim(payload[6:13], mine, own_active, axis=1)
    return corrector(terms, partial * gravity)


def solution(mesh):
    return jax.shard_map(
        on_device,
        mesh=mesh,
        in_specs=(
            P(None, ALL),
            P(None, ALL),
            P(None, ALL),
            P(None, ALL),
            P(ALL),
            P(ALL),
            P(ALL),
        ),
        out_specs=(
            P(None, ALL),
            P(None, ALL),
            P(None, ALL),
            P(None, ALL),
        ),
        check_vma=False,
    )
```

```python
import functools

import math

import jax
import jax.numpy as jnp
from jax import lax
from jax.experimental import pallas as pl
from jax.experimental.pallas import tpu as pltpu
from jax.sharding import PartitionSpec as P

softening = 0.001
ALL = ("blk", "group")
LEVELS = (("core", 1, 2), ("x", 2, 4), ("y_lo", 8, 2), ("z", 16, 4), ("y_hi", 64, 2))
FIELD_LEVELS = (("y_lo", 8, 2), ("core", 1, 2))
ACTIVE_LEVELS = (("y_hi", 64, 2), ("z", 16, 4), ("x", 2, 4))
SUB = 2


def predict(pos_now, vel_now, acc_now, jerk_now, elapsed):
    pred_pos = pos_now + elapsed * (
        vel_now + elapsed * (0.5 * acc_now + elapsed * (jerk_now / 6.0))
    )
    pred_vel = vel_now + elapsed * (acc_now + elapsed * (0.5 * jerk_now))
    return (pred_pos, pred_vel)


def corrector_terms(rows):
    old_pos = rows[0:3]
    old_vel = rows[3:6]
    old_acc = rows[6:9]
    old_jerk = rows[9:12]
    elapsed = rows[12]
    half = 0.5 * elapsed
    squared = elapsed * elapsed / 12.0
    vel_part = old_vel + half * old_acc + squared * old_jerk
    pos_part = old_pos + half * old_vel + squared * old_acc
    return jnp.concatenate([pos_part, vel_part, elapsed[None, :]], axis=0)


def corrector(terms, forces):
    pos_part = terms[0:3]
    vel_part = terms[3:6]
    elapsed = terms[6]
    new_acc = forces[0:3]
    new_jerk = forces[3:6]
    half = 0.5 * elapsed
    squared = elapsed * elapsed / 12.0
    new_vel = vel_part + half * new_acc - squared * new_jerk
    new_pos = pos_part + half * new_vel - squared * new_acc
    return (new_pos, new_vel, new_acc, new_jerk)


def _perm(stride, size, shift, ndev):
    pairs = []
    for d in range(ndev):
        c = (d // stride) % size
        pairs.append((d, d + (((c + shift) % size) - c) * stride))
    return pairs


def _coord(stride, size):
    return (lax.axis_index(ALL) // stride) % size


def gather_level(x, level, ndev):
    _, stride, size = level
    parts = [x] + [lax.ppermute(x, ALL, _perm(stride, size, s, ndev)) for s in range(1, size)]
    stack = jnp.stack(parts, axis=0)
    c = _coord(stride, size)
    order = (c - jnp.arange(size)) % size
    picked = jnp.take(stack, order, axis=0)
    picked = jnp.moveaxis(picked, 0, -2)
    return picked.reshape(x.shape[:-1] + (size * x.shape[-1],))


def reduce_level(x, level, ndev):
    _, stride, size = level
    m = x.shape[-1] // size
    blocks = x.reshape(x.shape[:-1] + (size, m))
    blocks = jnp.moveaxis(blocks, -2, 0)
    c = _coord(stride, size)
    total = jnp.take(blocks, c, axis=0)
    for s in range(1, size):
        piece = jnp.take(blocks, (c + s) % size, axis=0)
        total = total + lax.ppermute(piece, ALL, _perm(stride, size, s, ndev))
    return total


def sum_level(x, level, ndev):
    _, stride, size = level
    total = x
    for s in range(1, size):
        total = total + lax.ppermute(x, ALL, _perm(stride, size, s, ndev))
    return total


def forces_kernel(act_ref, fld_ref, out_ref, bfld, acc):
    num_k = act_ref.shape[0]
    num_j = fld_ref.shape[1]
    width = bfld.shape[2]
    step_k = 8 * SUB
    acc[...] = jnp.zeros(acc.shape, jnp.float32)

    def jblock(jb, carry):
        base = pl.multiple_of(jb * width, width)

        def spread(ci, c2):
            j0 = pl.multiple_of(ci * 128, 128)
            for c in range(7):
                row = fld_ref[c:c + 1, pl.ds(base + j0, 128)]
                bfld[c, :, pl.ds(j0, 128)] = jnp.broadcast_to(row, (8, 128))
            return c2

        lax.fori_loop(0, width // 128, spread, 0, unroll=4)

        def kblock(kb, c3):
            k0 = pl.multiple_of(kb * step_k, step_k)
            acts = []
            for s in range(SUB):
                a = act_ref[pl.ds(k0 + 8 * s, 8), :]
                acts.append([jnp.broadcast_to(a[:, c:c + 1], (8, 128)) for c in range(6)])

            def jstep(jc, accs):
                j0 = pl.multiple_of(jc * 128, 128)
                f = [bfld[c, :, pl.ds(j0, 128)] for c in range(7)]
                new = []
                for s in range(SUB):
                    ax, ay, az, avx, avy, avz = acts[s]
                    dx = f[0] - ax
                    dy = f[1] - ay
                    dz = f[2] - az
                    mx = f[3] - avx
                    my = f[4] - avy
                    mz = f[5] - avz
                    dist_sq = dx * dx + dy * dy + dz * dz + softening
                    inverse = lax.rsqrt(dist_sq)
                    inv2 = inverse * inverse
                    weight = f[6] * inv2 * inverse
                    factor = 3.0 * (dx * mx + dy * my + dz * mz) * inv2
                    a6 = accs[s]
                    new.append((
                        a6[0] + dx * weight,
                        a6[1] + dy * weight,
                        a6[2] + dz * weight,
                        a6[3] + (mx - factor * dx) * weight,
                        a6[4] + (my - factor * dy) * weight,
                        a6[5] + (mz - factor * dz) * weight,
                    ))
                return tuple(new)

            slot = kb * SUB
            init = tuple(tuple(acc[slot + s, c] for c in range(6)) for s in range(SUB))
            accs = lax.fori_loop(0, width // 128, jstep, init, unroll=16)
            for s in range(SUB):
                for c in range(6):
                    acc[slot + s, c] = accs[s][c]
            return c3

        lax.fori_loop(0, num_k // step_k, kblock, 0)
        return carry

    lax.fori_loop(0, num_j // width, jblock, 0)
    for kb in range(num_k // 8):
        for c in range(6):
            out_ref[pl.ds(8 * kb, 8), c:c + 1] = jnp.sum(acc[kb, c], axis=1, keepdims=True)


def pair_forces(active_t, field):
    num_k = active_t.shape[0]
    width = math.gcd(field.shape[1], 8192)
    return pl.pallas_call(
        forces_kernel,
        out_shape=jax.ShapeDtypeStruct((num_k, 8), jnp.float32),
        scratch_shapes=[
            pltpu.VMEM((7, 8, width), jnp.float32),
            pltpu.VMEM((num_k // 8, 6, 8, 128), jnp.float32),
        ],
    )(active_t, field)


def concat_level(x, level, ndev):
    _, stride, size = level
    parts = [x] + [lax.ppermute(x, ALL, _perm(stride, size, s, ndev)) for s in range(1, size)]
    return jnp.concatenate(parts, axis=-1)


def on_device(positions, velocities, accelerations, jerk_rates, masses, elapsed_time, active_index):
    ndev = lax.axis_size("blk") * lax.axis_size("group")
    own_stars = positions.shape[1]
    own_active = active_index.shape[0]
    total_stars = own_stars * ndev
    gravity = 1.0 / total_stars
    pred_pos, pred_vel = predict(positions, velocities, accelerations, jerk_rates, elapsed_time)
    field = jnp.concatenate([pred_pos, pred_vel, masses[None, :]], axis=0)
    for level in FIELD_LEVELS:
        field = concat_level(field, level, ndev)
    every_index = active_index
    for level in LEVELS:
        every_index = gather_level(every_index, level, ndev)
    packed = jnp.concatenate(
        [positions, velocities, accelerations, jerk_rates, elapsed_time[None, :]], axis=0
    )
    packed, field = lax.optimization_barrier((packed, field))
    first_row = lax.axis_index(ALL) * own_stars
    local_row = every_index - first_row
    is_owned = (local_row >= 0) & (local_row < own_stars)
    picked = jnp.take(packed, jnp.clip(local_row, 0, own_stars - 1), axis=1)
    picked = jnp.where(is_owned[None, :], picked, 0.0)
    act_pos, act_vel = predict(picked[0:3], picked[3:6], picked[6:9], picked[9:12], picked[12])
    payload = jnp.concatenate([act_pos, act_vel, corrector_terms(picked)], axis=0)
    rows = payload.shape[0]
    sizes = {name: size for name, _, size in LEVELS}
    order = ("y_hi", "z", "y_lo", "x", "core")
    payload = payload.reshape((rows,) + tuple(sizes[n] for n in order) + (own_active,))
    front = [order.index(n) + 1 for n, _, _ in FIELD_LEVELS]
    back = [order.index(n) + 1 for n, _, _ in ACTIVE_LEVELS]
    payload = payload.transpose([0] + front + back + [len(order) + 1]).reshape(rows, ndev * own_active)
    for level in FIELD_LEVELS:
        payload = reduce_level(payload, level, ndev)
    for level in ACTIVE_LEVELS:
        payload = sum_level(payload, level, ndev)
    num_k = payload.shape[1]
    active_t = jnp.concatenate([payload[0:6], jnp.zeros((2, num_k), jnp.float32)], axis=0).T
    partial = pair_forces(active_t, field)[:, 0:6].T
    for level in ACTIVE_LEVELS:
        partial = reduce_level(partial, level, ndev)
    mine = 0
    for _, stride, size in ACTIVE_LEVELS:
        mine = mine * size + _coord(stride, size)
    terms = lax.dynamic_slice_in_dim(payload[6:13], mine * own_active, own_active, axis=1)
    return corrector(terms, partial * gravity)


def solution(mesh):
    return jax.shard_map(
        on_device,
        mesh=mesh,
        in_specs=(
            P(None, ALL),
            P(None, ALL),
            P(None, ALL),
            P(None, ALL),
            P(ALL),
            P(ALL),
            P(ALL),
        ),
        out_specs=(
            P(None, ALL),
            P(None, ALL),
            P(None, ALL),
            P(None, ALL),
        ),
        check_vma=False,
    )
```

```python
import functools

import jax
import jax.numpy as jnp
from jax import lax
from jax.experimental import pallas as pl
from jax.experimental.pallas import tpu as pltpu
from jax.sharding import PartitionSpec as P

softening = 0.001
ALL = ("blk", "group")
LEVELS = (("core", 1, 2), ("x", 2, 4), ("y_lo", 8, 2), ("z", 16, 4), ("y_hi", 64, 2))
SUB = 2


def predict(pos_now, vel_now, acc_now, jerk_now, elapsed):
    pred_pos = pos_now + elapsed * (
        vel_now + elapsed * (0.5 * acc_now + elapsed * (jerk_now / 6.0))
    )
    pred_vel = vel_now + elapsed * (acc_now + elapsed * (0.5 * jerk_now))
    return (pred_pos, pred_vel)


def corrector_terms(rows):
    old_pos = rows[0:3]
    old_vel = rows[3:6]
    old_acc = rows[6:9]
    old_jerk = rows[9:12]
    elapsed = rows[12]
    half = 0.5 * elapsed
    squared = elapsed * elapsed / 12.0
    vel_part = old_vel + half * old_acc + squared * old_jerk
    pos_part = old_pos + half * old_vel + squared * old_acc
    return jnp.concatenate([pos_part, vel_part, elapsed[None, :]], axis=0)


def corrector(terms, forces):
    pos_part = terms[0:3]
    vel_part = terms[3:6]
    elapsed = terms[6]
    new_acc = forces[0:3]
    new_jerk = forces[3:6]
    half = 0.5 * elapsed
    squared = elapsed * elapsed / 12.0
    new_vel = vel_part + half * new_acc - squared * new_jerk
    new_pos = pos_part + half * new_vel - squared * new_acc
    return (new_pos, new_vel, new_acc, new_jerk)


def _perm(stride, size, shift, ndev):
    pairs = []
    for d in range(ndev):
        c = (d // stride) % size
        pairs.append((d, d + (((c + shift) % size) - c) * stride))
    return pairs


def _coord(stride, size):
    return (lax.axis_index(ALL) // stride) % size


def gather_level(x, level, ndev):
    _, stride, size = level
    parts = [x] + [lax.ppermute(x, ALL, _perm(stride, size, s, ndev)) for s in range(1, size)]
    stack = jnp.stack(parts, axis=0)
    c = _coord(stride, size)
    order = (c - jnp.arange(size)) % size
    picked = jnp.take(stack, order, axis=0)
    picked = jnp.moveaxis(picked, 0, -2)
    return picked.reshape(x.shape[:-1] + (size * x.shape[-1],))


def reduce_level(x, level, ndev):
    _, stride, size = level
    m = x.shape[-1] // size
    blocks = x.reshape(x.shape[:-1] + (size, m))
    blocks = jnp.moveaxis(blocks, -2, 0)
    c = _coord(stride, size)
    total = jnp.take(blocks, c, axis=0)
    for s in range(1, size):
        piece = jnp.take(blocks, (c + s) % size, axis=0)
        total = total + lax.ppermute(piece, ALL, _perm(stride, size, s, ndev))
    return total


def sum_level(x, level, ndev):
    _, stride, size = level
    total = x
    for s in range(1, size):
        total = total + lax.ppermute(x, ALL, _perm(stride, size, s, ndev))
    return total


def forces_kernel(act_ref, fld_ref, out_ref):
    num_k = act_ref.shape[0]
    num_j = fld_ref.shape[2]
    step_k = 8 * SUB

    def kblock(kb, carry):
        k0 = pl.multiple_of(kb * step_k, step_k)
        acts = []
        for s in range(SUB):
            a = act_ref[pl.ds(k0 + 8 * s, 8), :]
            acts.append([jnp.broadcast_to(a[:, c:c + 1], (8, 128)) for c in range(6)])

        def jstep(jc, accs):
            j0 = pl.multiple_of(jc * 128, 128)
            f = [fld_ref[c, :, pl.ds(j0, 128)] for c in range(7)]
            new = []
            for s in range(SUB):
                ax, ay, az, avx, avy, avz = acts[s]
                dx = f[0] - ax
                dy = f[1] - ay
                dz = f[2] - az
                mx = f[3] - avx
                my = f[4] - avy
                mz = f[5] - avz
                dist_sq = dx * dx + dy * dy + dz * dz + softening
                inverse = lax.rsqrt(dist_sq)
                inv2 = inverse * inverse
                weight = f[6] * inv2 * inverse
                factor = 3.0 * (dx * mx + dy * my + dz * mz) * inv2
                a6 = accs[s]
                new.append((
                    a6[0] + dx * weight,
                    a6[1] + dy * weight,
                    a6[2] + dz * weight,
                    a6[3] + (mx - factor * dx) * weight,
                    a6[4] + (my - factor * dy) * weight,
                    a6[5] + (mz - factor * dz) * weight,
                ))
            return tuple(new)

        zero = jnp.zeros((8, 128), jnp.float32)
        init = tuple(tuple(zero for _ in range(6)) for _ in range(SUB))
        accs = lax.fori_loop(0, num_j // 128, jstep, init, unroll=16)
        for s in range(SUB):
            for c in range(6):
                out_ref[pl.ds(k0 + 8 * s, 8), pl.ds(c * 128, 128)] = accs[s][c]
        return carry

    lax.fori_loop(0, num_k // step_k, kblock, 0)


def pair_forces(active_t, field_b):
    num_k = active_t.shape[0]
    return pl.pallas_call(
        forces_kernel,
        out_shape=jax.ShapeDtypeStruct((num_k, 6 * 128), jnp.float32),
    )(active_t, field_b)


def on_device(positions, velocities, accelerations, jerk_rates, masses, elapsed_time, active_index):
    ndev = lax.axis_size("blk") * lax.axis_size("group")
    own_stars = positions.shape[1]
    total_stars = own_stars * ndev
    gravity = 1.0 / total_stars
    every_index = active_index
    for level in LEVELS:
        every_index = gather_level(every_index, level, ndev)
    pred_pos, pred_vel = predict(positions, velocities, accelerations, jerk_rates, elapsed_time)
    own_field = jnp.concatenate(
        [pred_pos, pred_vel, masses[None, :], jnp.zeros_like(masses)[None, :]], axis=0
    )
    field_b = jnp.broadcast_to(own_field[:, None, :], (8, 8, own_stars))
    packed = jnp.concatenate(
        [positions, velocities, accelerations, jerk_rates, elapsed_time[None, :]], axis=0
    )
    first_row = lax.axis_index(ALL) * own_stars
    local_row = every_index - first_row
    is_owned = (local_row >= 0) & (local_row < own_stars)
    picked = jnp.take(packed, jnp.clip(local_row, 0, own_stars - 1), axis=1)
    picked = jnp.where(is_owned[None, :], picked, 0.0)
    act_pos, act_vel = predict(picked[0:3], picked[3:6], picked[6:9], picked[9:12], picked[12])
    num_k = picked.shape[1]
    active = jnp.concatenate([act_pos, act_vel], axis=0)
    for level in LEVELS:
        active = sum_level(active, level, ndev)
    active_t = jnp.concatenate([active, jnp.zeros((2, num_k), jnp.float32)], axis=0).T
    partial = jnp.sum(pair_forces(active_t, field_b).reshape(num_k, 6, 128), axis=2).T
    payload = jnp.concatenate([partial, corrector_terms(picked)], axis=0)
    for level in reversed(LEVELS):
        payload = reduce_level(payload, level, ndev)
    return corrector(payload[6:13], payload[0:6] * gravity)


def solution(mesh):
    return jax.shard_map(
        on_device,
        mesh=mesh,
        in_specs=(
            P(None, ALL),
            P(None, ALL),
            P(None, ALL),
            P(None, ALL),
            P(ALL),
            P(ALL),
            P(ALL),
        ),
        out_specs=(
            P(None, ALL),
            P(None, ALL),
            P(None, ALL),
            P(None, ALL),
        ),
        check_vma=False,
    )
```

```python
import functools

import jax
import jax.numpy as jnp
from jax import lax
from jax.experimental import pallas as pl
from jax.experimental.pallas import tpu as pltpu
from jax.sharding import PartitionSpec as P

softening = 0.001
ALL = ("blk", "group")
LEVELS = (("core", 1, 2), ("x", 2, 4), ("y_lo", 8, 2), ("z", 16, 4), ("y_hi", 64, 2))
SUB = 2


def predict(pos_now, vel_now, acc_now, jerk_now, elapsed):
    pred_pos = pos_now + elapsed * (
        vel_now + elapsed * (0.5 * acc_now + elapsed * (jerk_now / 6.0))
    )
    pred_vel = vel_now + elapsed * (acc_now + elapsed * (0.5 * jerk_now))
    return (pred_pos, pred_vel)


def corrector_terms(rows):
    old_pos = rows[0:3]
    old_vel = rows[3:6]
    old_acc = rows[6:9]
    old_jerk = rows[9:12]
    elapsed = rows[12]
    half = 0.5 * elapsed
    squared = elapsed * elapsed / 12.0
    vel_part = old_vel + half * old_acc + squared * old_jerk
    pos_part = old_pos + half * old_vel + squared * old_acc
    return jnp.concatenate([pos_part, vel_part, elapsed[None, :]], axis=0)


def corrector(terms, forces):
    pos_part = terms[0:3]
    vel_part = terms[3:6]
    elapsed = terms[6]
    new_acc = forces[0:3]
    new_jerk = forces[3:6]
    half = 0.5 * elapsed
    squared = elapsed * elapsed / 12.0
    new_vel = vel_part + half * new_acc - squared * new_jerk
    new_pos = pos_part + half * new_vel - squared * new_acc
    return (new_pos, new_vel, new_acc, new_jerk)


def _perm(stride, size, shift, ndev):
    pairs = []
    for d in range(ndev):
        c = (d // stride) % size
        pairs.append((d, d + (((c + shift) % size) - c) * stride))
    return pairs


def _coord(stride, size):
    return (lax.axis_index(ALL) // stride) % size


def gather_level(x, level, ndev):
    _, stride, size = level
    parts = [x] + [lax.ppermute(x, ALL, _perm(stride, size, s, ndev)) for s in range(1, size)]
    stack = jnp.stack(parts, axis=0)
    c = _coord(stride, size)
    order = (c - jnp.arange(size)) % size
    picked = jnp.take(stack, order, axis=0)
    picked = jnp.moveaxis(picked, 0, -2)
    return picked.reshape(x.shape[:-1] + (size * x.shape[-1],))


def reduce_level(x, level, ndev):
    _, stride, size = level
    m = x.shape[-1] // size
    blocks = x.reshape(x.shape[:-1] + (size, m))
    blocks = jnp.moveaxis(blocks, -2, 0)
    c = _coord(stride, size)
    total = jnp.take(blocks, c, axis=0)
    for s in range(1, size):
        piece = jnp.take(blocks, (c + s) % size, axis=0)
        total = total + lax.ppermute(piece, ALL, _perm(stride, size, s, ndev))
    return total


def sum_level(x, level, ndev):
    _, stride, size = level
    total = x
    for s in range(1, size):
        total = total + lax.ppermute(x, ALL, _perm(stride, size, s, ndev))
    return total


def forces_kernel(act_ref, fld_ref, out_ref):
    num_k = act_ref.shape[0]
    num_j = fld_ref.shape[2]
    step_k = 8 * SUB

    def kblock(kb, carry):
        k0 = pl.multiple_of(kb * step_k, step_k)
        acts = []
        for s in range(SUB):
            a = act_ref[pl.ds(k0 + 8 * s, 8), :]
            acts.append([jnp.broadcast_to(a[:, c:c + 1], (8, 128)) for c in range(6)])

        def jstep(jc, accs):
            j0 = pl.multiple_of(jc * 128, 128)
            f = [fld_ref[c, :, pl.ds(j0, 128)] for c in range(7)]
            new = []
            for s in range(SUB):
                ax, ay, az, avx, avy, avz = acts[s]
                dx = f[0] - ax
                dy = f[1] - ay
                dz = f[2] - az
                mx = f[3] - avx
                my = f[4] - avy
                mz = f[5] - avz
                dist_sq = dx * dx + dy * dy + dz * dz + softening
                inverse = lax.rsqrt(dist_sq)
                inv2 = inverse * inverse
                weight = f[6] * inv2 * inverse
                factor = 3.0 * (dx * mx + dy * my + dz * mz) * inv2
                a6 = accs[s]
                new.append((
                    a6[0] + dx * weight,
                    a6[1] + dy * weight,
                    a6[2] + dz * weight,
                    a6[3] + (mx - factor * dx) * weight,
                    a6[4] + (my - factor * dy) * weight,
                    a6[5] + (mz - factor * dz) * weight,
                ))
            return tuple(new)

        zero = jnp.zeros((8, 128), jnp.float32)
        init = tuple(tuple(zero for _ in range(6)) for _ in range(SUB))
        accs = lax.fori_loop(0, num_j // 128, jstep, init, unroll=16)
        for s in range(SUB):
            for c in range(6):
                out_ref[c, pl.ds(k0 + 8 * s, 8), :] = accs[s][c]
        return carry

    lax.fori_loop(0, num_k // step_k, kblock, 0)


def pair_forces(active_t, field_b):
    num_k = active_t.shape[0]
    return pl.pallas_call(
        forces_kernel,
        out_shape=jax.ShapeDtypeStruct((6, num_k, 128), jnp.float32),
    )(active_t, field_b)


def on_device(positions, velocities, accelerations, jerk_rates, masses, elapsed_time, active_index):
    ndev = lax.axis_size("blk") * lax.axis_size("group")
    own_stars = positions.shape[1]
    total_stars = own_stars * ndev
    gravity = 1.0 / total_stars
    every_index = active_index
    for level in LEVELS:
        every_index = gather_level(every_index, level, ndev)
    pred_pos, pred_vel = predict(positions, velocities, accelerations, jerk_rates, elapsed_time)
    own_field = jnp.concatenate(
        [pred_pos, pred_vel, masses[None, :], jnp.zeros_like(masses)[None, :]], axis=0
    )
    field_b = jnp.broadcast_to(own_field[:, None, :], (8, 8, own_stars))
    packed = jnp.concatenate(
        [positions, velocities, accelerations, jerk_rates, elapsed_time[None, :]], axis=0
    )
    first_row = lax.axis_index(ALL) * own_stars
    local_row = every_index - first_row
    is_owned = (local_row >= 0) & (local_row < own_stars)
    picked = jnp.take(packed, jnp.clip(local_row, 0, own_stars - 1), axis=1)
    picked = jnp.where(is_owned[None, :], picked, 0.0)
    act_pos, act_vel = predict(picked[0:3], picked[3:6], picked[6:9], picked[9:12], picked[12])
    num_k = picked.shape[1]
    active = jnp.concatenate([act_pos, act_vel], axis=0)
    for level in LEVELS:
        active = sum_level(active, level, ndev)
    active_t = jnp.concatenate([active, jnp.zeros((2, num_k), jnp.float32)], axis=0).T
    partial = jnp.sum(pair_forces(active_t, field_b), axis=2)
    payload = jnp.concatenate([partial, corrector_terms(picked)], axis=0)
    for level in reversed(LEVELS):
        payload = reduce_level(payload, level, ndev)
    return corrector(payload[6:13], payload[0:6] * gravity)


def solution(mesh):
    return jax.shard_map(
        on_device,
        mesh=mesh,
        in_specs=(
            P(None, ALL),
            P(None, ALL),
            P(None, ALL),
            P(None, ALL),
            P(ALL),
            P(ALL),
            P(ALL),
        ),
        out_specs=(
            P(None, ALL),
            P(None, ALL),
            P(None, ALL),
            P(None, ALL),
        ),
        check_vma=False,
    )
```

```python
import jax
import jax.numpy as jnp
from jax import lax
from jax.experimental import pallas as pl
from jax.sharding import PartitionSpec as P


softening = 0.001
ALL = ("blk", "group")
LEVELS = (("core", 1, 2), ("x", 2, 4), ("y_lo", 8, 2), ("z", 16, 4), ("y_hi", 64, 2))
SUB = 2


def predict(pos_now, vel_now, acc_now, jerk_now, elapsed):
    pred_pos = pos_now + elapsed * (
        vel_now + elapsed * (0.5 * acc_now + elapsed * (jerk_now / 6.0))
    )
    pred_vel = vel_now + elapsed * (acc_now + elapsed * (0.5 * jerk_now))
    return (pred_pos, pred_vel)


def corrector_terms(rows):
    old_pos = rows[0:3]
    old_vel = rows[3:6]
    old_acc = rows[6:9]
    old_jerk = rows[9:12]
    elapsed = rows[12]
    half = 0.5 * elapsed
    squared = elapsed * elapsed / 12.0
    vel_part = old_vel + half * old_acc + squared * old_jerk
    pos_part = old_pos + half * old_vel + squared * old_acc
    return jnp.concatenate([pos_part, vel_part, elapsed[None, :]], axis=0)


def corrector(terms, forces):
    pos_part = terms[0:3]
    vel_part = terms[3:6]
    elapsed = terms[6]
    new_acc = forces[0:3]
    new_jerk = forces[3:6]
    half = 0.5 * elapsed
    squared = elapsed * elapsed / 12.0
    new_vel = vel_part + half * new_acc - squared * new_jerk
    new_pos = pos_part + half * new_vel - squared * new_acc
    return (new_pos, new_vel, new_acc, new_jerk)


def _perm(stride, size, shift, ndev):
    pairs = []
    for d in range(ndev):
        c = (d // stride) % size
        pairs.append((d, d + (((c + shift) % size) - c) * stride))
    return pairs


def _coord(stride, size):
    return (lax.axis_index(ALL) // stride) % size


def gather_level(x, level, ndev):
    _, stride, size = level
    parts = [x] + [lax.ppermute(x, ALL, _perm(stride, size, s, ndev)) for s in range(1, size)]
    stack = jnp.stack(parts, axis=0)
    c = _coord(stride, size)
    order = (c - jnp.arange(size)) % size
    picked = jnp.take(stack, order, axis=0)
    picked = jnp.moveaxis(picked, 0, -2)
    return picked.reshape(x.shape[:-1] + (size * x.shape[-1],))


def reduce_level(x, level, ndev):
    _, stride, size = level
    m = x.shape[-1] // size
    blocks = x.reshape(x.shape[:-1] + (size, m))
    blocks = jnp.moveaxis(blocks, -2, 0)
    c = _coord(stride, size)
    total = jnp.take(blocks, c, axis=0)
    for s in range(1, size):
        piece = jnp.take(blocks, (c + s) % size, axis=0)
        total = total + lax.ppermute(piece, ALL, _perm(stride, size, s, ndev))
    return total


def sum_level(x, level, ndev):
    _, stride, size = level
    total = x
    for s in range(1, size):
        total = total + lax.ppermute(x, ALL, _perm(stride, size, s, ndev))
    return total


def forces_kernel(act_ref, fld_ref, out_ref):
    num_k = act_ref.shape[0]
    num_j = fld_ref.shape[2]
    step_k = 8 * SUB

    def kblock(kb, carry):
        k0 = pl.multiple_of(kb * step_k, step_k)
        acts = []
        for s in range(SUB):
            a = act_ref[pl.ds(k0 + 8 * s, 8), :]
            acts.append([jnp.broadcast_to(a[:, c:c + 1], (8, 128)) for c in range(6)])

        def jstep(jc, accs):
            j0 = pl.multiple_of(jc * 128, 128)
            f = [fld_ref[c, :, pl.ds(j0, 128)] for c in range(7)]
            new = []
            for s in range(SUB):
                ax, ay, az, avx, avy, avz = acts[s]
                dx = f[0] - ax
                dy = f[1] - ay
                dz = f[2] - az
                mx = f[3] - avx
                my = f[4] - avy
                mz = f[5] - avz
                dist_sq = dx * dx + dy * dy + dz * dz + softening
                inverse = lax.rsqrt(dist_sq)
                inv2 = inverse * inverse
                weight = f[6] * inv2 * inverse
                factor = 3.0 * (dx * mx + dy * my + dz * mz) * inv2
                a6 = accs[s]
                new.append((
                    a6[0] + dx * weight,
                    a6[1] + dy * weight,
                    a6[2] + dz * weight,
                    a6[3] + (mx - factor * dx) * weight,
                    a6[4] + (my - factor * dy) * weight,
                    a6[5] + (mz - factor * dz) * weight,
                ))
            return tuple(new)

        zero = jnp.zeros((8, 128), jnp.float32)
        init = tuple(tuple(zero for _ in range(6)) for _ in range(SUB))
        accs = lax.fori_loop(0, num_j // 128, jstep, init, unroll=16)
        for s in range(SUB):
            for c in range(6):
                out_ref[c, pl.ds(k0 + 8 * s, 8), :] = accs[s][c]
        return carry

    lax.fori_loop(0, num_k // step_k, kblock, 0)


def pair_forces(active_t, field_b):
    num_k = active_t.shape[0]
    return pl.pallas_call(
        forces_kernel,
        out_shape=jax.ShapeDtypeStruct((6, num_k, 128), jnp.float32),
    )(active_t, field_b)


def step(positions, velocities, accelerations, jerk_rates, masses, elapsed_time, active_index):
    ndev = lax.axis_size("blk") * lax.axis_size("group")
    own_stars = positions.shape[1]
    total_stars = own_stars * ndev
    gravity = 1.0 / total_stars
    every_index = active_index
    for level in LEVELS:
        every_index = gather_level(every_index, level, ndev)
    pred_pos, pred_vel = predict(positions, velocities, accelerations, jerk_rates, elapsed_time)
    own_field = jnp.concatenate(
        [pred_pos, pred_vel, masses[None, :], jnp.zeros_like(masses)[None, :]], axis=0
    )
    field_b = jnp.broadcast_to(own_field[:, None, :], (8, 8, own_stars))
    packed = jnp.concatenate(
        [positions, velocities, accelerations, jerk_rates, elapsed_time[None, :]], axis=0
    )
    first_row = lax.axis_index(ALL) * own_stars
    local_row = every_index - first_row
    is_owned = (local_row >= 0) & (local_row < own_stars)
    picked = jnp.take(packed, jnp.clip(local_row, 0, own_stars - 1), axis=1)
    picked = jnp.where(is_owned[None, :], picked, 0.0)
    act_pos, act_vel = predict(picked[0:3], picked[3:6], picked[6:9], picked[9:12], picked[12])
    num_k = picked.shape[1]
    active = jnp.concatenate([act_pos, act_vel], axis=0)
    for level in LEVELS:
        active = sum_level(active, level, ndev)
    active_t = jnp.concatenate([active, jnp.zeros((2, num_k), jnp.float32)], axis=0).T
    terms = corrector_terms(picked)
    _, stride, size = LEVELS[-1]
    half = num_k // size
    upper = _coord(stride, size)
    send_at = ((upper + 1) % size) * half
    keep_at = upper * half

    def half_payload(start):
        act = lax.dynamic_slice_in_dim(active_t, start, half, axis=0)
        part = jnp.sum(pair_forces(act, field_b), axis=2)
        return jnp.concatenate([part, lax.dynamic_slice_in_dim(terms, start, half, axis=1)], axis=0)

    sent = lax.ppermute(half_payload(send_at), ALL, _perm(stride, size, 1, ndev))
    payload = half_payload(keep_at) + sent
    for level in reversed(LEVELS[:-1]):
        payload = reduce_level(payload, level, ndev)
    return corrector(payload[6:13], payload[0:6] * gravity)


def solution(mesh):
    return jax.shard_map(
        step,
        mesh=mesh,
        in_specs=(
            P(None, ALL),
            P(None, ALL),
            P(None, ALL),
            P(None, ALL),
            P(ALL),
            P(ALL),
            P(ALL),
        ),
        out_specs=(
            P(None, ALL),
            P(None, ALL),
            P(None, ALL),
            P(None, ALL),
        ),
        check_vma=False,
    )
```

```python
import jax
import jax.numpy as jnp
from jax import lax
from jax.experimental import pallas as pl
from jax.sharding import PartitionSpec as P


softening = 0.001
ALL = ("blk", "group")
LEVELS = (("core", 1, 2), ("x", 2, 4), ("y_lo", 8, 2), ("z", 16, 4), ("y_hi", 64, 2))
SUB = 2


def predict(pos_now, vel_now, acc_now, jerk_now, elapsed):
    pred_pos = pos_now + elapsed * (
        vel_now + elapsed * (0.5 * acc_now + elapsed * (jerk_now / 6.0))
    )
    pred_vel = vel_now + elapsed * (acc_now + elapsed * (0.5 * jerk_now))
    return (pred_pos, pred_vel)


def corrector_terms(rows):
    old_pos = rows[0:3]
    old_vel = rows[3:6]
    old_acc = rows[6:9]
    old_jerk = rows[9:12]
    elapsed = rows[12]
    half = 0.5 * elapsed
    squared = elapsed * elapsed / 12.0
    vel_part = old_vel + half * old_acc + squared * old_jerk
    pos_part = old_pos + half * old_vel + squared * old_acc
    return jnp.concatenate([pos_part, vel_part, elapsed[None, :]], axis=0)


def corrector(terms, forces):
    pos_part = terms[0:3]
    vel_part = terms[3:6]
    elapsed = terms[6]
    new_acc = forces[0:3]
    new_jerk = forces[3:6]
    half = 0.5 * elapsed
    squared = elapsed * elapsed / 12.0
    new_vel = vel_part + half * new_acc - squared * new_jerk
    new_pos = pos_part + half * new_vel - squared * new_acc
    return (new_pos, new_vel, new_acc, new_jerk)


def _perm(stride, size, shift, ndev):
    pairs = []
    for d in range(ndev):
        c = (d // stride) % size
        pairs.append((d, d + (((c + shift) % size) - c) * stride))
    return pairs


def _coord(stride, size):
    return (lax.axis_index(ALL) // stride) % size


def gather_level(x, level, ndev):
    _, stride, size = level
    parts = [x] + [lax.ppermute(x, ALL, _perm(stride, size, s, ndev)) for s in range(1, size)]
    stack = jnp.stack(parts, axis=0)
    c = _coord(stride, size)
    order = (c - jnp.arange(size)) % size
    picked = jnp.take(stack, order, axis=0)
    picked = jnp.moveaxis(picked, 0, -2)
    return picked.reshape(x.shape[:-1] + (size * x.shape[-1],))


def reduce_level(x, level, ndev):
    _, stride, size = level
    m = x.shape[-1] // size
    blocks = x.reshape(x.shape[:-1] + (size, m))
    blocks = jnp.moveaxis(blocks, -2, 0)
    c = _coord(stride, size)
    total = jnp.take(blocks, c, axis=0)
    for s in range(1, size):
        piece = jnp.take(blocks, (c + s) % size, axis=0)
        total = total + lax.ppermute(piece, ALL, _perm(stride, size, s, ndev))
    return total


def sum_level(x, level, ndev):
    _, stride, size = level
    total = x
    for s in range(1, size):
        total = total + lax.ppermute(x, ALL, _perm(stride, size, s, ndev))
    return total


def forces_kernel(act_ref, fld_ref, out_ref):
    num_k = act_ref.shape[0]
    num_j = fld_ref.shape[2]
    step_k = 8 * SUB

    def kblock(kb, carry):
        k0 = pl.multiple_of(kb * step_k, step_k)
        acts = []
        for s in range(SUB):
            a = act_ref[pl.ds(k0 + 8 * s, 8), :]
            acts.append([jnp.broadcast_to(a[:, c:c + 1], (8, 128)) for c in range(6)])

        def jstep(jc, accs):
            j0 = pl.multiple_of(jc * 128, 128)
            f = [fld_ref[c, :, pl.ds(j0, 128)] for c in range(7)]
            new = []
            for s in range(SUB):
                ax, ay, az, avx, avy, avz = acts[s]
                dx = f[0] - ax
                dy = f[1] - ay
                dz = f[2] - az
                mx = f[3] - avx
                my = f[4] - avy
                mz = f[5] - avz
                dist_sq = dx * dx + dy * dy + dz * dz + softening
                inverse = lax.rsqrt(dist_sq)
                inv2 = inverse * inverse
                weight = f[6] * inv2 * inverse
                factor = 3.0 * (dx * mx + dy * my + dz * mz) * inv2
                a6 = accs[s]
                new.append((
                    a6[0] + dx * weight,
                    a6[1] + dy * weight,
                    a6[2] + dz * weight,
                    a6[3] + (mx - factor * dx) * weight,
                    a6[4] + (my - factor * dy) * weight,
                    a6[5] + (mz - factor * dz) * weight,
                ))
            return tuple(new)

        zero = jnp.zeros((8, 128), jnp.float32)
        init = tuple(tuple(zero for _ in range(6)) for _ in range(SUB))
        accs = lax.fori_loop(0, num_j // 128, jstep, init, unroll=32)
        for s in range(SUB):
            for c in range(6):
                out_ref[c, pl.ds(k0 + 8 * s, 8), :] = accs[s][c]
        return carry

    lax.fori_loop(0, num_k // step_k, kblock, 0)


def pair_forces(active_t, field_b):
    num_k = active_t.shape[0]
    return pl.pallas_call(
        forces_kernel,
        out_shape=jax.ShapeDtypeStruct((6, num_k, 128), jnp.float32),
    )(active_t, field_b)


def step(positions, velocities, accelerations, jerk_rates, masses, elapsed_time, active_index):
    ndev = lax.axis_size("blk") * lax.axis_size("group")
    own_stars = positions.shape[1]
    total_stars = own_stars * ndev
    gravity = 1.0 / total_stars
    every_index = active_index
    for level in LEVELS[:-1]:
        every_index = gather_level(every_index, level, ndev)
    _, last_stride, last_size = LEVELS[-1]
    other_index = lax.ppermute(every_index, ALL, _perm(last_stride, last_size, 1, ndev))
    pred_pos, pred_vel = predict(positions, velocities, accelerations, jerk_rates, elapsed_time)
    own_field = jnp.concatenate(
        [pred_pos, pred_vel, masses[None, :], jnp.zeros_like(masses)[None, :]], axis=0
    )
    field_b = jnp.broadcast_to(own_field[:, None, :], (8, 8, own_stars))
    packed = jnp.concatenate(
        [positions, velocities, accelerations, jerk_rates, elapsed_time[None, :]], axis=0
    )
    first_row = lax.axis_index(ALL) * own_stars

    def pick(index):
        local_row = index - first_row
        is_owned = (local_row >= 0) & (local_row < own_stars)
        rows = jnp.take(packed, jnp.clip(local_row, 0, own_stars - 1), axis=1)
        return jnp.where(is_owned[None, :], rows, 0.0)

    own_half = pick(every_index)
    other_half = pick(other_index)
    picked = jnp.where(
        _coord(last_stride, last_size) == 1,
        jnp.concatenate([other_half, own_half], axis=1),
        jnp.concatenate([own_half, other_half], axis=1),
    )
    act_pos, act_vel = predict(picked[0:3], picked[3:6], picked[6:9], picked[9:12], picked[12])
    num_k = picked.shape[1]
    active = jnp.concatenate([act_pos, act_vel], axis=0)
    for level in LEVELS:
        active = sum_level(active, level, ndev)
    active_t = jnp.concatenate([active, jnp.zeros((2, num_k), jnp.float32)], axis=0).T
    partial = jnp.sum(pair_forces(active_t, field_b), axis=2)
    payload = jnp.concatenate([partial, corrector_terms(picked)], axis=0)
    for level in reversed(LEVELS):
        payload = reduce_level(payload, level, ndev)
    return corrector(payload[6:13], payload[0:6] * gravity)


def solution(mesh):
    return jax.shard_map(
        step,
        mesh=mesh,
        in_specs=(
            P(None, ALL),
            P(None, ALL),
            P(None, ALL),
            P(None, ALL),
            P(ALL),
            P(ALL),
            P(ALL),
        ),
        out_specs=(
            P(None, ALL),
            P(None, ALL),
            P(None, ALL),
            P(None, ALL),
        ),
        check_vma=False,
    )
```

```python
import jax
import jax.numpy as jnp
from jax import lax
from jax.experimental import pallas as pl
from jax.sharding import PartitionSpec as P


softening = 0.001
ALL = ("blk", "group")
LEVELS = (("core", 1, 2), ("x", 2, 4), ("y_lo", 8, 2), ("z", 16, 4), ("y_hi", 64, 2))
SUB = 2


def predict(pos_now, vel_now, acc_now, jerk_now, elapsed):
    pred_pos = pos_now + elapsed * (
        vel_now + elapsed * (0.5 * acc_now + elapsed * (jerk_now / 6.0))
    )
    pred_vel = vel_now + elapsed * (acc_now + elapsed * (0.5 * jerk_now))
    return (pred_pos, pred_vel)


def corrector_terms(rows):
    old_pos = rows[0:3]
    old_vel = rows[3:6]
    old_acc = rows[6:9]
    old_jerk = rows[9:12]
    elapsed = rows[12]
    half = 0.5 * elapsed
    squared = elapsed * elapsed / 12.0
    vel_part = old_vel + half * old_acc + squared * old_jerk
    pos_part = old_pos + half * old_vel + squared * old_acc
    return jnp.concatenate([pos_part, vel_part, elapsed[None, :]], axis=0)


def corrector(terms, forces):
    pos_part = terms[0:3]
    vel_part = terms[3:6]
    elapsed = terms[6]
    new_acc = forces[0:3]
    new_jerk = forces[3:6]
    half = 0.5 * elapsed
    squared = elapsed * elapsed / 12.0
    new_vel = vel_part + half * new_acc - squared * new_jerk
    new_pos = pos_part + half * new_vel - squared * new_acc
    return (new_pos, new_vel, new_acc, new_jerk)


def _perm(stride, size, shift, ndev):
    pairs = []
    for d in range(ndev):
        c = (d // stride) % size
        pairs.append((d, d + (((c + shift) % size) - c) * stride))
    return pairs


def _coord(stride, size):
    return (lax.axis_index(ALL) // stride) % size


def gather_level(x, level, ndev):
    _, stride, size = level
    parts = [x] + [lax.ppermute(x, ALL, _perm(stride, size, s, ndev)) for s in range(1, size)]
    stack = jnp.stack(parts, axis=0)
    c = _coord(stride, size)
    order = (c - jnp.arange(size)) % size
    picked = jnp.take(stack, order, axis=0)
    picked = jnp.moveaxis(picked, 0, -2)
    return picked.reshape(x.shape[:-1] + (size * x.shape[-1],))


def reduce_level(x, level, ndev):
    _, stride, size = level
    m = x.shape[-1] // size
    blocks = x.reshape(x.shape[:-1] + (size, m))
    blocks = jnp.moveaxis(blocks, -2, 0)
    c = _coord(stride, size)
    total = jnp.take(blocks, c, axis=0)
    for s in range(1, size):
        piece = jnp.take(blocks, (c + s) % size, axis=0)
        total = total + lax.ppermute(piece, ALL, _perm(stride, size, s, ndev))
    return total


def sum_level(x, level, ndev):
    _, stride, size = level
    total = x
    for s in range(1, size):
        total = total + lax.ppermute(x, ALL, _perm(stride, size, s, ndev))
    return total


def forces_kernel(act_ref, fld_ref, out_ref):
    num_k = act_ref.shape[0]
    num_j = fld_ref.shape[2]
    step_k = 8 * SUB

    def kblock(kb, carry):
        k0 = pl.multiple_of(kb * step_k, step_k)
        acts = []
        for s in range(SUB):
            a = act_ref[pl.ds(k0 + 8 * s, 8), :]
            acts.append([jnp.broadcast_to(a[:, c:c + 1], (8, 128)) for c in range(6)])

        def jstep(jc, accs):
            j0 = pl.multiple_of(jc * 128, 128)
            f = [fld_ref[c, :, pl.ds(j0, 128)] for c in range(7)]
            new = []
            for s in range(SUB):
                ax, ay, az, avx, avy, avz = acts[s]
                dx = f[0] - ax
                dy = f[1] - ay
                dz = f[2] - az
                mx = f[3] - avx
                my = f[4] - avy
                mz = f[5] - avz
                dist_sq = dx * dx + dy * dy + dz * dz + softening
                inverse = lax.rsqrt(dist_sq)
                inv2 = inverse * inverse
                weight = f[6] * inv2 * inverse
                factor = 3.0 * (dx * mx + dy * my + dz * mz) * inv2
                a6 = accs[s]
                new.append((
                    a6[0] + dx * weight,
                    a6[1] + dy * weight,
                    a6[2] + dz * weight,
                    a6[3] + (mx - factor * dx) * weight,
                    a6[4] + (my - factor * dy) * weight,
                    a6[5] + (mz - factor * dz) * weight,
                ))
            return tuple(new)

        zero = jnp.zeros((8, 128), jnp.float32)
        init = tuple(tuple(zero for _ in range(6)) for _ in range(SUB))
        accs = lax.fori_loop(0, num_j // 128, jstep, init, unroll=64)
        for s in range(SUB):
            for c in range(6):
                out_ref[c, pl.ds(k0 + 8 * s, 8), :] = accs[s][c]
        return carry

    lax.fori_loop(0, num_k // step_k, kblock, 0, unroll=4)


def pair_forces(active_t, field_b):
    num_k = active_t.shape[0]
    return pl.pallas_call(
        forces_kernel,
        out_shape=jax.ShapeDtypeStruct((6, num_k, 128), jnp.float32),
    )(active_t, field_b)


def step(positions, velocities, accelerations, jerk_rates, masses, elapsed_time, active_index):
    ndev = lax.axis_size("blk") * lax.axis_size("group")
    own_stars = positions.shape[1]
    total_stars = own_stars * ndev
    gravity = 1.0 / total_stars
    every_index = active_index
    for level in LEVELS:
        every_index = gather_level(every_index, level, ndev)
    pred_pos, pred_vel = predict(positions, velocities, accelerations, jerk_rates, elapsed_time)
    own_field = jnp.concatenate(
        [pred_pos, pred_vel, masses[None, :], jnp.zeros_like(masses)[None, :]], axis=0
    )
    field_b = jnp.broadcast_to(own_field[:, None, :], (8, 8, own_stars))
    packed = jnp.concatenate(
        [positions, velocities, accelerations, jerk_rates, elapsed_time[None, :]], axis=0
    )
    first_row = lax.axis_index(ALL) * own_stars
    local_row = every_index - first_row
    is_owned = (local_row >= 0) & (local_row < own_stars)
    picked = jnp.take(packed, jnp.clip(local_row, 0, own_stars - 1), axis=1)
    picked = jnp.where(is_owned[None, :], picked, 0.0)
    act_pos, act_vel = predict(picked[0:3], picked[3:6], picked[6:9], picked[9:12], picked[12])
    num_k = picked.shape[1]
    active = jnp.concatenate([act_pos, act_vel], axis=0)
    for level in LEVELS:
        active = sum_level(active, level, ndev)
    active_t = jnp.concatenate([active, jnp.zeros((2, num_k), jnp.float32)], axis=0).T
    partial = jnp.sum(pair_forces(active_t, field_b), axis=2)
    payload = jnp.concatenate([partial, corrector_terms(picked)], axis=0)
    for level in reversed(LEVELS):
        payload = reduce_level(payload, level, ndev)
    return corrector(payload[6:13], payload[0:6] * gravity)


def solution(mesh):
    return jax.shard_map(
        step,
        mesh=mesh,
        in_specs=(
            P(None, ALL),
            P(None, ALL),
            P(None, ALL),
            P(None, ALL),
            P(ALL),
            P(ALL),
            P(ALL),
        ),
        out_specs=(
            P(None, ALL),
            P(None, ALL),
            P(None, ALL),
            P(None, ALL),
        ),
        check_vma=False,
    )
```
